128 devices in a mesh: req: 8 (over y_lo, x), exp: 16 (over y_hi, z, core).
Axes of the slice: x: 4, y: 4 (y_hi: 2, y_lo: 2; y = y_hi * 2 + y_lo), z: 4, core: 2. Of those that a mesh axis runs over, the one named last changes fastest.
Arguments:
- hidden: bfloat16 [16384, 2048], P(('req', 'exp')), may hold values from -6 to 6
- norm_attn: float32 [2048], replicated, may hold values from 0.1 to 1.9
- qkv_weight: bfloat16 [3, 2048, 2048], P(None, None, 'exp'), may hold values from -0.21875 to 0.21875
- out_weight: bfloat16 [2048, 2048], P('exp'), may hold values from -0.375 to 0.375
- prefix_pool: bfloat16 [8, 64, 16, 4096], P('req', 'exp'), may hold values from -112 to 112, as said below
- page_table: int32 [8, 32], P('req'), may hold values from 0 to 63, as said below
- suffix_lengths: int32 [8, 2], P('req'), may hold values from 1 to 1536, 2048 in all within a row
- norm_moe: float32 [2048], replicated, may hold values from 0.1 to 1.9
- routes: int32 [16384, 8], P(('req', 'exp')), may hold values from 0 to 63, all different within a row; in each aligned block of 128 rows (0 to 127, 128 to 255, ...) at most 20 rows name the same one
- route_weights: float32 [16384, 8], P(('req', 'exp')), may hold values from 0.25 to 1
- expert_gate: bfloat16 [128, 2048, 512], P(('req', 'exp')), may hold values from -0.125 to 0.125
- expert_up: bfloat16 [128, 2048, 512], P(('req', 'exp')), may hold values from -0.125 to 0.125
- expert_down: bfloat16 [128, 512, 2048], P(('req', 'exp')), may hold values from -0.1875 to 0.1875
Outputs:
- layer_out: bfloat16 [16384, 2048], P(('req', 'exp'))
- suffix_keys: bfloat16 [16384, 2048], P('req', 'exp')
- suffix_values: bfloat16 [16384, 2048], P('req', 'exp')
The draws below stay inside these ranges and needn't reach their ends.
Inputs may be any that keep to these rules, and one draw needn't show every extreme that they name: `prefix_pool`: prefix keys and values; half of each head's slot holds the key, half the value. `page_table`: each row names 32 different pages of its group's pool, exactly half of each aligned block of 4 pages. `routes`: among the rows of one device no expert is named more than 20 times, a bound that some block reaches by the rows of one device.
All inputs are finite; a program needn't handle non-finite values.
Results may differ from the reference program's by a relative error of at most 0.02.
The reference program's roundings to bfloat16 on the way count: a program that leaves them out, or rounds other values in their place, can miss the bound.
Values may be sent and summed in bfloat16 or wider, within the bound.
No kernel may reach another device: no remote copies, remote signals or barrier semaphores. Data moves between devices by JAX's collectives and lax.ppermute only.
A program may use at most 192 MiB of HBM per device.

```python
import math
import jax
import jax.numpy as jnp
import numpy as np
from jax import lax

D = 2048
HEADS = 16
HD = 128
FFE = 1024
TOPK = 8
PAGE = 16
REQS = 2
TOK_DEV = 128
POOL_DEV = 4
EXPERTS = 64
FFH = 512
GT = 2048
TOKENS = 16384
POOL = 64
PREFIX = 512
CAP = 20
REQ_MOST = 1536
N_EXP = 16


def draw_prefix_pool(key, part):
    groups = TOKENS // GT
    shape = (groups, POOL, PAGE, HEADS, 2, HD)
    filled = 1.5 * jax.random.truncated_normal(key, -4.0, 4.0, shape, jnp.float32)
    return filled.reshape(groups, POOL, PAGE, 2 * HEADS * HD).astype(jnp.bfloat16)


def draw_page_table(key, part):
    groups = TOKENS // GT
    owners = POOL // POOL_DEV
    half_size = POOL_DEV // 2

    def one_group(group_key):
        keys_all = jax.random.split(group_key, owners + 1)
        local = jax.vmap(lambda owner_key: jax.random.permutation(owner_key, POOL_DEV)[:half_size])(keys_all[:owners])
        row_base = (jnp.arange(owners, dtype=jnp.int32) * POOL_DEV)[:, None]
        flat_pages = (local.astype(jnp.int32) + row_base).reshape(-1)
        return jax.random.permutation(keys_all[owners], flat_pages)
    return jax.vmap(one_group)(jax.random.split(key, groups)).astype(jnp.int32)


def block_scale(key, extent, cuts, low, high):
    gain, own = 1.0, jax.random.fold_in(key, 6)
    for dim, parts in cuts:
        draws = jnp.exp(jax.random.uniform(jax.random.fold_in(own, dim), (parts,), jnp.float32, low / len(cuts), high / len(cuts)))
        gain = gain * jnp.repeat(draws, extent[dim] // parts).reshape([-1 if axis == dim else 1 for axis in range(len(extent))])
    return gain


def split_up(amount, total, reach, lean):
    weights = [(1 << 20) // math.isqrt(grade ** lean) + 1 for grade in range(2, amount + 1)]
    surplus, counts = total - reach - (amount - 1), [1] * (amount - 1)
    while surplus > 0:
        free = [i for i in range(amount - 1) if counts[i] < reach]
        pool, left = sum([weights[i] for i in free]), surplus
        for i in free:
            extra = min(reach - counts[i], max(1, left * weights[i] // pool), surplus)
            counts[i] = counts[i] + extra
            surplus = surplus - extra
    return np.array([reach] + counts)


def uneven_parts(key, number_of, total, bound, slope):
    if number_of == 2:
        one = jax.random.randint(key, (), max(1, total - bound), min(bound, total - 1) + 1)
        return jnp.stack([one, total - one])
    sizes = jnp.asarray(split_up(number_of, total, bound, slope), jnp.int32)
    couples = (number_of - 1) // 2
    source_of, receiver = sizes[1:1 + 2 * couples:2], sizes[2:2 + 2 * couples:2]
    slack = jnp.minimum(source_of - 1, bound - receiver)
    moved = jax.random.randint(jax.random.fold_in(key, 1), (couples,), 0, 1 << 20) % (slack + 1)
    sizes = sizes.at[1:1 + 2 * couples:2].set(source_of - moved).at[2:2 + 2 * couples:2].set(receiver + moved)
    return sizes[jax.random.permutation(jax.random.fold_in(key, 2), number_of)]


def deal_out(key, own, number, rows, count, top, reach, lean):
    order = jax.random.permutation(key, count)
    crowded, common = load_shares(count, rows * top, reach, lean, True), load_shares(count, rows * top, reach, lean, False)
    places = jnp.arange(count)

    def named(lengths, rotation):
        used = int((lengths > 0).sum())
        fixed = max(1, used // 4)
        passed = fixed + (places - fixed + rotation * (used - fixed)) % max(1, count - fixed)
        return jnp.zeros((count,), jnp.int32).at[order[jnp.where(places < fixed, places, passed)]].set(jnp.asarray(lengths, jnp.int32))

    lengths = jnp.where(number % 4 == 0, named(crowded, number // 4), named(common, number - number // 4 - 1))
    mixed = jax.random.permutation(jax.random.fold_in(own, 3), count)
    giver, sink = mixed[0:count // 2 * 2:2], mixed[1:count // 2 * 2:2]
    slack = jnp.minimum(lengths[giver] - 1, reach - lengths[sink]) // 2
    slack = jnp.where((giver == order[0]) | (sink == order[0]) | (lengths[sink] == 0), 0, jnp.maximum(slack, 0))
    passed = jax.random.randint(jax.random.fold_in(own, 4), (count // 2,), 0, 1 << 20) % (slack + 1)
    lengths = lengths.at[giver].add(-passed).at[sink].add(passed)
    members = jnp.searchsorted(jnp.cumsum(lengths), jnp.arange(rows * top), side="right").astype(jnp.int32)
    listing = members.reshape(top, rows).T
    listing = listing[jax.random.permutation(jax.random.fold_in(own, 1), rows)]
    rotation = jax.random.randint(jax.random.fold_in(own, 2), (rows, 1), 0, top)
    return jnp.take_along_axis(listing, (jnp.arange(top)[None, :] + rotation) % top, axis=1)


def load_shares(count, total, most, lean, full):
    loads = [(1 << 20) // math.isqrt(rank ** lean) + 1 for rank in range(1, count + 1)]
    largest = most if full else min(most, max(-(-total // count), total * loads[0] // sum(loads)))
    least = 1 if total - largest >= count - 1 else 0
    holding, surplus = [largest] + [least] * (count - 1), total - largest - least * (count - 1)
    while surplus > 0:
        candidates = [i for i in range(1, count) if holding[i] < largest] or [i for i in range(1, count) if holding[i] < most]
        whole, budget = sum([loads[i] for i in candidates]), surplus
        for i in candidates:
            more = min(most - holding[i], max(1, budget * loads[i] // whole), surplus)
            holding[i] = holding[i] + more
            surplus = surplus - more
    return np.array(holding)


def bell_draw(rng, shape, deviation, reach, pieces=(), kind=jnp.bfloat16):
    values = jax.random.normal(rng, shape, jnp.float32) * deviation
    if len(pieces) > 0:
        values = block_scale(rng, shape, pieces, -0.22, 0.18) * values
    return jnp.clip(values, min=-reach, max=reach).astype(kind)


def setup_inputs(seed: int = 0) -> dict:
    key_list = jax.random.split(jax.random.key(seed), 14)
    hidden = bell_draw(key_list[0], (TOKENS, D), 1.0, 6.0, ((0, 128),))
    norm_attn = jnp.clip(1.0 + 0.18 * jax.random.normal(key_list[1], (D,), jnp.float32), 0.1, 1.9)
    qkv_weight = bell_draw(key_list[2], (3, D, HEADS * HD), (D // 3) ** -0.5, 0.21875, ((2, 16),))
    out_weight = bell_draw(key_list[3], (HEADS * HD, D), (HEADS * HD // 9) ** -0.5, 0.375, ((0, 16),))
    prefix_pool = draw_prefix_pool(jax.random.fold_in(key_list[13], 71), 0)
    page_table = draw_page_table(jax.random.fold_in(key_list[13], 71), 0)
    suffix_lengths = jax.vmap(lambda own: uneven_parts(own, REQS, GT, REQ_MOST, 2))(jax.random.split(key_list[6], (TOKENS // GT))).reshape((TOKENS // GT, REQS)).astype(jnp.int32)
    norm_moe = jnp.clip(1.0 + 0.18 * jax.random.normal(key_list[7], (D,), jnp.float32), 0.1, 1.9)
    routes_keys = jax.random.split(jax.random.fold_in(key_list[8], 1), TOKENS // TOK_DEV)
    routes_turns = jax.random.permutation(jax.random.fold_in(key_list[8], 3), TOKENS // TOK_DEV)
    routes = jax.vmap(lambda own, number: deal_out(jax.random.fold_in(key_list[8], 2), own, number, TOK_DEV, EXPERTS, TOPK, CAP, 2))(routes_keys, routes_turns).reshape((TOKENS, TOPK))
    route_weights = jnp.clip(0.25 + 0.75 * jax.random.uniform(key_list[9], (TOKENS, TOPK), jnp.float32) ** block_scale(key_list[9], (TOKENS, TOPK), ((0, 128),), -0.2, 0.2), 0.25, 1.0)
    expert_gate = bell_draw(key_list[10], (2 * EXPERTS, D, FFH), D ** -0.5, 0.125, ((0, 128),))
    expert_up = bell_draw(key_list[11], (2 * EXPERTS, D, FFH), D ** -0.5, 0.125, ((0, 128),))
    expert_down = bell_draw(key_list[12], (2 * EXPERTS, FFH, D), FFE ** -0.5, 0.1875, ((0, 128),))
    return dict(hidden=hidden, norm_attn=norm_attn, qkv_weight=qkv_weight, out_weight=out_weight, prefix_pool=prefix_pool, page_table=page_table, suffix_lengths=suffix_lengths, norm_moe=norm_moe, routes=routes, route_weights=route_weights, expert_gate=expert_gate, expert_up=expert_up, expert_down=expert_down)


eps_norm = 1e-06
rope_base = 10000.0

def rms_scale(inputs, gains_vec):
    return inputs * lax.rsqrt(lax.optimization_barrier(jnp.mean(inputs * inputs, axis=-1, keepdims=True)) + eps_norm) * gains_vec

def positions_of(group_lengths, tok_count, offset):
    end_marks = jnp.cumsum(group_lengths).astype(jnp.int32)
    places = jnp.arange(tok_count, dtype=jnp.int32)
    request = lax.optimization_barrier(jnp.sum((places[:, None] >= end_marks[None, :]).astype(jnp.int32), axis=1)).astype(jnp.int32)
    starts = end_marks - group_lengths
    onehot = (request[:, None] == jnp.arange(group_lengths.shape[0], dtype=jnp.int32)[None, :]).astype(jnp.int32)
    first_place = lax.optimization_barrier(jnp.sum(onehot * starts[None, :], axis=1)).astype(jnp.int32)
    return (request, places - first_place + offset)

def rotate(inputs, places):
    half_size = inputs.shape[-1] // 2
    frequency = rope_base ** (-jnp.arange(half_size, dtype=jnp.float32) * 2.0 / inputs.shape[-1])
    angles = places.astype(jnp.float32)[:, None] * frequency[None, :]
    cosine = jnp.cos(angles)[:, None, :]
    sine_part = jnp.sin(angles)[:, None, :]
    lower = inputs[..., :half_size]
    upper = inputs[..., half_size:]
    return jnp.concatenate([lower * cosine - upper * sine_part, upper * cosine + lower * sine_part], axis=-1)

def place_routes(block_routes):
    flat_routes = block_routes.reshape(-1)
    onehot = (flat_routes[:, None] == jnp.arange(EXPERTS, dtype=jnp.int32)[None, :]).astype(jnp.int32)
    before = jnp.cumsum(onehot, axis=0).astype(jnp.int32) - onehot
    slot_rank = lax.optimization_barrier(jnp.sum(before * onehot, axis=1)).astype(jnp.int32)
    return flat_routes * CAP + slot_rank

def attend(operands):
    queries, key_rows, value_rows, prefix_keys, prefix_values, same_request = operands
    score_scale = HD ** (-0.5)
    prefix_scores = jnp.dot(queries, prefix_keys.T, preferred_element_type=jnp.float32) * score_scale
    suffix_scores = jnp.dot(queries, key_rows.T, preferred_element_type=jnp.float32) * score_scale
    suffix_scores = jnp.where(same_request, suffix_scores, -1e+30)
    row_max = jnp.maximum(lax.optimization_barrier(jnp.max(prefix_scores, axis=1, keepdims=True)), lax.optimization_barrier(jnp.max(suffix_scores, axis=1, keepdims=True)))
    prefix_weights = jnp.exp(prefix_scores - row_max)
    suffix_weights = jnp.exp(suffix_scores - row_max)
    denominator = lax.optimization_barrier(jnp.sum(prefix_weights, axis=1, keepdims=True)) + lax.optimization_barrier(jnp.sum(suffix_weights, axis=1, keepdims=True))
    weighted = jnp.dot(prefix_weights.astype(jnp.bfloat16), prefix_values, preferred_element_type=jnp.float32)
    weighted = weighted + jnp.dot(suffix_weights.astype(jnp.bfloat16), value_rows, preferred_element_type=jnp.float32)
    return (weighted / denominator).astype(jnp.bfloat16)

def reference(hidden, norm_attn, qkv_weight, out_weight, prefix_pool, page_table, suffix_lengths, norm_moe, routes, route_weights, expert_gate, expert_up, expert_down):
    head_width = HEADS * HD
    groups = TOKENS // GT
    hidden_f = hidden.astype(jnp.float32)
    normed = rms_scale(hidden_f, norm_attn).astype(jnp.bfloat16)
    stacked = jnp.transpose(qkv_weight, (1, 0, 2)).reshape(D, 3 * head_width)
    projected = jnp.dot(normed, stacked, preferred_element_type=jnp.float32).reshape(TOKENS, 3, HEADS, HD)
    request_ids, places = jax.vmap(lambda group_lengths: positions_of(group_lengths, GT, PREFIX))(suffix_lengths)
    queries = rotate(projected[:, 0], places.reshape(TOKENS)).astype(jnp.bfloat16)
    key_rows = rotate(projected[:, 1], places.reshape(TOKENS)).astype(jnp.bfloat16)
    value_rows = projected[:, 2].astype(jnp.bfloat16)
    page_data = prefix_pool.reshape(groups, POOL, PAGE, HEADS, 2, HD)
    query_groups = queries.reshape(groups, GT, HEADS, HD)
    key_groups = key_rows.reshape(groups, GT, HEADS, HD)
    value_groups = value_rows.reshape(groups, GT, HEADS, HD)

    def one_group(group_index):
        group_queries = lax.dynamic_index_in_dim(query_groups, group_index, 0, keepdims=False)
        group_keys = lax.dynamic_index_in_dim(key_groups, group_index, 0, keepdims=False)
        group_values = lax.dynamic_index_in_dim(value_groups, group_index, 0, keepdims=False)
        group_pool = lax.dynamic_index_in_dim(page_data, group_index, 0, keepdims=False)
        page_rows = lax.dynamic_index_in_dim(page_table, group_index, 0, keepdims=False)
        live_prefix = jnp.take(group_pool, page_rows, axis=0).reshape(PREFIX, HEADS, 2, HD)
        group_requests = lax.dynamic_index_in_dim(request_ids, group_index, 0, keepdims=False)
        same_request = group_requests[:, None] == group_requests[None, :]

        def one_head(operands):
            return attend(operands + (same_request,))
        return lax.map(one_head, (jnp.transpose(group_queries, (1, 0, 2)), jnp.transpose(group_keys, (1, 0, 2)), jnp.transpose(group_values, (1, 0, 2)), jnp.transpose(live_prefix[:, :, 0], (1, 0, 2)), jnp.transpose(live_prefix[:, :, 1], (1, 0, 2))))
    heads_out = lax.map(one_group, jnp.arange(groups, dtype=jnp.int32))
    heads_out = jnp.transpose(heads_out, (0, 2, 1, 3)).reshape(TOKENS, head_width)
    part_width = head_width // N_EXP
    attn_sum = jnp.zeros((TOKENS, D), jnp.float32)
    for part_index in range(N_EXP):
        partial_sum = jnp.dot(heads_out[:, part_index * part_width:(part_index + 1) * part_width], out_weight[part_index * part_width:(part_index + 1) * part_width], preferred_element_type=jnp.float32)
        rounded = lax.optimization_barrier(partial_sum.astype(jnp.bfloat16))
        attn_sum = attn_sum + rounded.astype(jnp.float32)
    residual = hidden_f + attn_sum
    normed_moe = rms_scale(residual, norm_moe).astype(jnp.bfloat16)
    devices = TOKENS // TOK_DEV
    slot_of = jax.vmap(place_routes)(routes.reshape(devices, TOK_DEV, TOPK))
    owners = jnp.repeat(jnp.arange(TOK_DEV, dtype=jnp.int32), TOPK)

    def fill_table(slots_one, weights_one):
        owner_table = jnp.zeros((EXPERTS * CAP,), jnp.int32).at[slots_one].set(owners)
        weight_table = jnp.zeros((EXPERTS * CAP,), jnp.float32).at[slots_one].set(weights_one)
        return (owner_table, weight_table)
    owner_table, weight_table = jax.vmap(fill_table)(slot_of, route_weights.reshape(devices, TOK_DEV * TOPK))
    row_base = (jnp.arange(devices, dtype=jnp.int32) * TOK_DEV)[:, None]

    def one_expert(moe_sum, expert):
        slot_rows = lax.dynamic_slice_in_dim(owner_table, expert * CAP, CAP, 1) + row_base
        slot_gains = lax.dynamic_slice_in_dim(weight_table, expert * CAP, CAP, 1).reshape(-1)
        flat_rows = slot_rows.reshape(-1)
        inputs = jnp.take(normed_moe, flat_rows, axis=0)
        result = jnp.zeros((flat_rows.shape[0], D), jnp.float32)
        for half_index in range(2):
            index = 2 * expert + half_index
            gate_proj = jnp.dot(inputs, lax.dynamic_index_in_dim(expert_gate, index, 0, keepdims=False), preferred_element_type=jnp.float32)
            up_proj = jnp.dot(inputs, lax.dynamic_index_in_dim(expert_up, index, 0, keepdims=False), preferred_element_type=jnp.float32)
            activated = (jax.nn.silu(gate_proj) * up_proj).astype(jnp.bfloat16)
            half_out = jnp.dot(activated, lax.dynamic_index_in_dim(expert_down, index, 0, keepdims=False), preferred_element_type=jnp.float32).astype(jnp.bfloat16)
            result = result + half_out.astype(jnp.float32)
        return (moe_sum.at[flat_rows].add(slot_gains[:, None] * result), None)
    moe_sum, _ = lax.scan(one_expert, jnp.zeros((TOKENS, D), jnp.float32), jnp.arange(EXPERTS, dtype=jnp.int32))
    layer_out = (residual + moe_sum).astype(jnp.bfloat16)
    return (layer_out, key_rows.reshape(TOKENS, head_width), value_rows.reshape(TOKENS, head_width))
```

```python
import jax
import jax.numpy as jnp
from jax import lax
from jax.sharding import PartitionSpec as P

HD = 128
PAGE = 16


eps_norm = 1e-06
rope_base = 10000.0


def rms_scale(inputs, gains_vec):
    return (
        inputs * lax.rsqrt(jnp.mean(inputs * inputs, axis=-1, keepdims=True) + eps_norm) * gains_vec
    )


def positions_of(group_lengths, tok_count, offset):
    end_marks = jnp.cumsum(group_lengths)
    places = jnp.arange(tok_count, dtype=jnp.int32)
    request = jnp.sum((places[:, None] >= end_marks[None, :]).astype(jnp.int32), axis=1)
    starts = end_marks - group_lengths
    onehot = (
        request[:, None] == jnp.arange(group_lengths.shape[0], dtype=jnp.int32)[None, :]
    ).astype(jnp.int32)
    first_place = jnp.sum(onehot * starts[None, :], axis=1)
    return (request, places - first_place + offset)


def rotate(inputs, places):
    half_size = inputs.shape[-1] // 2
    frequency = rope_base ** (-jnp.arange(half_size, dtype=jnp.float32) * 2.0 / inputs.shape[-1])
    angles = places.astype(jnp.float32)[:, None] * frequency[None, :]
    cosine = jnp.cos(angles)[:, None, :]
    sine_part = jnp.sin(angles)[:, None, :]
    lower = inputs[..., :half_size]
    upper = inputs[..., half_size:]
    return jnp.concatenate(
        [lower * cosine - upper * sine_part, upper * cosine + lower * sine_part], axis=-1
    )


def place_routes(block_routes, expert_count, capacity):
    flat_routes = block_routes.reshape(-1)
    entries = flat_routes.shape[0]
    onehot = (flat_routes[:, None] == jnp.arange(expert_count, dtype=jnp.int32)[None, :]).astype(
        jnp.bfloat16
    )
    rows_i = jnp.arange(entries, dtype=jnp.int32)
    earlier = (rows_i[None, :] < rows_i[:, None]).astype(jnp.bfloat16)
    before = jnp.dot(earlier, onehot, preferred_element_type=jnp.float32)
    slot_rank = jnp.sum(before * onehot.astype(jnp.float32), axis=1).astype(jnp.int32)
    return flat_routes * capacity + slot_rank


def half_apply(flat_rows, gate_mat, up_mat, down_mat):
    gate_proj = jnp.dot(flat_rows, gate_mat, preferred_element_type=jnp.float32)
    up_proj = jnp.dot(flat_rows, up_mat, preferred_element_type=jnp.float32)
    activated = (jax.nn.silu(gate_proj) * up_proj).astype(jnp.bfloat16)
    return jnp.dot(activated, down_mat, preferred_element_type=jnp.float32).astype(jnp.bfloat16)


def on_device(
    hidden,
    norm_attn,
    qkv_weight,
    out_weight,
    prefix_pool,
    page_table,
    suffix_lengths,
    norm_moe,
    routes,
    route_weights,
    expert_gate,
    expert_up,
    expert_down,
):
    tok_rows, model_width = hidden.shape
    holders = lax.axis_size("exp")
    head_dim = HD
    local_width = qkv_weight.shape[2]
    local_heads = local_width // head_dim
    partner = [(i, i ^ 1) for i in range(holders)]
    other_gate = lax.ppermute(expert_gate[0], "exp", partner)
    other_up = lax.ppermute(expert_up[0], "exp", partner)
    other_down = lax.ppermute(expert_down[0], "exp", partner)
    hidden_f = hidden.astype(jnp.float32)
    normed = rms_scale(hidden_f, norm_attn).astype(jnp.bfloat16)
    projected = jnp.einsum(
        "rd,cdh->rch",
        lax.all_gather(normed, "exp", axis=0, tiled=True),
        qkv_weight,
        preferred_element_type=jnp.float32,
    )
    group_rows = projected.shape[0]
    prefix_len = page_table.shape[1] * PAGE
    request, places = positions_of(suffix_lengths[0], group_rows, prefix_len)
    projected = projected.reshape(group_rows, 3, local_heads, head_dim)
    queries = rotate(projected[:, 0], places).astype(jnp.bfloat16)
    key_rows = rotate(projected[:, 1], places).astype(jnp.bfloat16)
    value_rows = projected[:, 2].astype(jnp.bfloat16)
    page_rows = page_table[0]
    page_data = lax.all_to_all(prefix_pool, "exp", split_axis=3, concat_axis=1, tiled=True)
    all_slots = jnp.arange(page_data.shape[1], dtype=jnp.int32)
    used_mask = jnp.sum((page_rows[None, :] == all_slots[:, None]).astype(jnp.int32), axis=1) > 0
    prefix_ok = jnp.repeat(used_mask, PAGE)
    page_data = page_data.reshape(-1, local_heads, 2, head_dim)
    prefix_keys = page_data[:, :, 0]
    prefix_values = page_data[:, :, 1]
    score_scale = head_dim ** (-0.5)
    block_rows = min(512, group_rows)
    block_count = group_rows // block_rows

    def block_attend(operands):
        block_queries, block_requests = operands
        prefix_scores = (
            jnp.einsum(
                "qhd,khd->hqk", block_queries, prefix_keys, preferred_element_type=jnp.float32
            )
            * score_scale
        )
        prefix_scores = jnp.where(prefix_ok[None, None, :], prefix_scores, -1e30)
        suffix_scores = (
            jnp.einsum("qhd,khd->hqk", block_queries, key_rows, preferred_element_type=jnp.float32)
            * score_scale
        )
        same_request = block_requests[:, None] == request[None, :]
        suffix_scores = jnp.where(same_request[None], suffix_scores, -1e30)
        row_max = jnp.maximum(
            jnp.max(prefix_scores, axis=2, keepdims=True),
            jnp.max(suffix_scores, axis=2, keepdims=True),
        )
        prefix_weights = jnp.exp(prefix_scores - row_max)
        suffix_weights = jnp.exp(suffix_scores - row_max)
        denominator = jnp.sum(prefix_weights, axis=2) + jnp.sum(suffix_weights, axis=2)
        weighted = jnp.einsum(
            "hqk,khd->qhd",
            prefix_weights.astype(jnp.bfloat16),
            prefix_values,
            preferred_element_type=jnp.float32,
        )
        weighted = weighted + jnp.einsum(
            "hqk,khd->qhd",
            suffix_weights.astype(jnp.bfloat16),
            value_rows,
            preferred_element_type=jnp.float32,
        )
        return (weighted / jnp.transpose(denominator)[:, :, None]).astype(jnp.bfloat16)

    attended = lax.map(
        block_attend,
        (
            queries.reshape(block_count, block_rows, local_heads, head_dim),
            request.reshape(block_count, block_rows),
        ),
    )
    heads_out = attended.reshape(group_rows, local_width)
    token_heads = lax.all_to_all(
        heads_out.reshape(holders, tok_rows, local_width), "exp", split_axis=0, concat_axis=0,
        tiled=True,
    )
    full_out_weight = lax.all_gather(out_weight, "exp", axis=0, tiled=True)
    attn_sum = jnp.zeros((tok_rows, model_width), jnp.float32)
    for part_index in range(holders):
        partial_sum = jnp.dot(
            token_heads[part_index],
            full_out_weight[part_index * local_width:(part_index + 1) * local_width],
            preferred_element_type=jnp.float32,
        )
        attn_sum = attn_sum + partial_sum.astype(jnp.bfloat16).astype(jnp.float32)
    residual = hidden_f + attn_sum
    normed_moe = rms_scale(residual, norm_moe).astype(jnp.bfloat16)
    req_count = lax.axis_size("req")
    expert_count = req_count * holders // 2
    route_count = routes.shape[1]
    capacity = max(2, tok_rows * route_count * 5 // (4 * expert_count))
    assert capacity % 2 == 0
    slot_total = expert_count * capacity
    slot_of = place_routes(routes, expert_count, capacity)
    slot_hits = (slot_of[:, None] == jnp.arange(slot_total, dtype=jnp.int32)[None, :]).reshape(
        tok_rows, route_count, slot_total
    )
    dispatch = jnp.sum(slot_hits.astype(jnp.int32), axis=1).astype(jnp.bfloat16)
    send_rows = jnp.einsum(
        "ts,td->sd", dispatch, normed_moe, preferred_element_type=jnp.float32
    ).astype(jnp.bfloat16)
    send_rows = send_rows.reshape(2 * expert_count, capacity // 2, model_width)
    arrived = lax.all_to_all(send_rows, ("req", "exp"), split_axis=0, concat_axis=0, tiled=True)
    lead_shape = arrived.shape[:-1]
    flat_rows = arrived.reshape(-1, model_width)
    mine = half_apply(flat_rows, expert_gate[0], expert_up[0], expert_down[0])
    other = half_apply(flat_rows, other_gate, other_up, other_down)
    both = (mine.astype(jnp.float32) + other.astype(jnp.float32)).astype(jnp.bfloat16)
    returned = lax.all_to_all(
        both.reshape(lead_shape + (model_width,)),
        ("req", "exp"),
        split_axis=0,
        concat_axis=0,
        tiled=True,
    )
    slot_values = returned.reshape(slot_total, model_width).astype(jnp.float32)
    combine = jnp.sum(
        slot_hits.astype(jnp.float32) * route_weights[:, :, None], axis=1
    )
    moe_sum = jnp.dot(
        combine, slot_values, precision=lax.Precision.HIGHEST, preferred_element_type=jnp.float32
    )
    layer_out = (residual + moe_sum).astype(jnp.bfloat16)
    return (
        layer_out,
        key_rows.reshape(group_rows, local_width),
        value_rows.reshape(group_rows, local_width),
    )


def solution(mesh):
    return jax.shard_map(
        on_device,
        mesh=mesh,
        in_specs=(
            P(("req", "exp"), None),
            P(),
            P(None, None, "exp"),
            P("exp", None),
            P("req", "exp", None, None),
            P("req", None),
            P("req", None),
            P(),
            P(("req", "exp"), None),
            P(("req", "exp"), None),
            P(("req", "exp"), None, None),
            P(("req", "exp"), None, None),
            P(("req", "exp"), None, None),
        ),
        out_specs=(P(("req", "exp"), None), P("req", "exp"), P("req", "exp")),
        check_vma=False,
    )
```

```python
import jax
import jax.numpy as jnp
from jax import lax
from jax.sharding import PartitionSpec as P

HD = 128
PAGE = 16


eps_norm = 1e-06
rope_base = 10000.0


def rms_scale(inputs, gains_vec):
    return (
        inputs * lax.rsqrt(jnp.mean(inputs * inputs, axis=-1, keepdims=True) + eps_norm) * gains_vec
    )


def positions_of(group_lengths, tok_count, offset):
    end_marks = jnp.cumsum(group_lengths)
    places = jnp.arange(tok_count, dtype=jnp.int32)
    request = jnp.sum((places[:, None] >= end_marks[None, :]).astype(jnp.int32), axis=1)
    starts = end_marks - group_lengths
    onehot = (
        request[:, None] == jnp.arange(group_lengths.shape[0], dtype=jnp.int32)[None, :]
    ).astype(jnp.int32)
    first_place = jnp.sum(onehot * starts[None, :], axis=1)
    return (request, places - first_place + offset)


def rotate(inputs, places):
    half_size = inputs.shape[-1] // 2
    frequency = rope_base ** (-jnp.arange(half_size, dtype=jnp.float32) * 2.0 / inputs.shape[-1])
    angles = places.astype(jnp.float32)[:, None] * frequency[None, :]
    cosine = jnp.cos(angles)[:, None, :]
    sine_part = jnp.sin(angles)[:, None, :]
    lower = inputs[..., :half_size]
    upper = inputs[..., half_size:]
    return jnp.concatenate(
        [lower * cosine - upper * sine_part, upper * cosine + lower * sine_part], axis=-1
    )


def place_routes(block_routes, expert_count, capacity):
    flat_routes = block_routes.reshape(-1)
    entries = flat_routes.shape[0]
    onehot = (flat_routes[:, None] == jnp.arange(expert_count, dtype=jnp.int32)[None, :]).astype(
        jnp.bfloat16
    )
    rows_i = jnp.arange(entries, dtype=jnp.int32)
    earlier = (rows_i[None, :] < rows_i[:, None]).astype(jnp.bfloat16)
    before = jnp.dot(earlier, onehot, preferred_element_type=jnp.float32)
    slot_rank = jnp.sum(before * onehot.astype(jnp.float32), axis=1).astype(jnp.int32)
    return flat_routes * capacity + slot_rank


def aligned_block(size):
    for rows in (16, 8):
        if size % (rows * 128) == 0:
            return (rows, size // rows)
    return (1, size)


def half_apply(flat_rows, gate_mat, up_mat, down_mat):
    gate_proj = jnp.dot(flat_rows, gate_mat, preferred_element_type=jnp.float32)
    up_proj = jnp.dot(flat_rows, up_mat, preferred_element_type=jnp.float32)
    activated = (jax.nn.silu(gate_proj) * up_proj).astype(jnp.bfloat16)
    return jnp.dot(activated, down_mat, preferred_element_type=jnp.float32).astype(jnp.bfloat16)


def on_device(
    hidden,
    norm_attn,
    qkv_weight,
    out_weight,
    prefix_pool,
    page_table,
    suffix_lengths,
    norm_moe,
    routes,
    route_weights,
    expert_gate,
    expert_up,
    expert_down,
):
    tok_rows, model_width = hidden.shape
    holders = lax.axis_size("exp")
    head_dim = HD
    local_width = qkv_weight.shape[2]
    local_heads = local_width // head_dim
    partner = [(i, i ^ 1) for i in range(holders)]
    other_gate = lax.ppermute(expert_gate[0], "exp", partner)
    other_up = lax.ppermute(expert_up[0], "exp", partner)
    other_down = lax.ppermute(expert_down[0], "exp", partner)
    hidden_f = hidden.astype(jnp.float32)
    normed = rms_scale(hidden_f, norm_attn).astype(jnp.bfloat16)
    projected = jnp.einsum(
        "rd,cdh->rch",
        lax.all_gather(normed, "exp", axis=0, tiled=True),
        qkv_weight,
        preferred_element_type=jnp.float32,
    )
    group_rows = projected.shape[0]
    prefix_len = page_table.shape[1] * PAGE
    request, places = positions_of(suffix_lengths[0], group_rows, prefix_len)
    projected = projected.reshape(group_rows, 3, local_heads, head_dim)
    queries = rotate(projected[:, 0], places).astype(jnp.bfloat16)
    key_rows = rotate(projected[:, 1], places).astype(jnp.bfloat16)
    value_rows = projected[:, 2].astype(jnp.bfloat16)
    page_rows = page_table[0]
    page_data = lax.all_to_all(prefix_pool, "exp", split_axis=3, concat_axis=1, tiled=True)
    all_slots = jnp.arange(page_data.shape[1], dtype=jnp.int32)
    used_mask = jnp.sum((page_rows[None, :] == all_slots[:, None]).astype(jnp.int32), axis=1) > 0
    prefix_ok = jnp.repeat(used_mask, PAGE)
    page_data = page_data.reshape(-1, local_heads, 2, head_dim)
    prefix_keys = page_data[:, :, 0]
    prefix_values = page_data[:, :, 1]
    score_scale = head_dim ** (-0.5)
    block_rows = min(512, group_rows)
    block_count = group_rows // block_rows

    def block_attend(operands):
        block_queries, block_requests = operands
        prefix_scores = (
            jnp.einsum(
                "qhd,khd->hqk", block_queries, prefix_keys, preferred_element_type=jnp.float32
            )
            * score_scale
        )
        prefix_scores = jnp.where(prefix_ok[None, None, :], prefix_scores, -1e30)
        suffix_scores = (
            jnp.einsum("qhd,khd->hqk", block_queries, key_rows, preferred_element_type=jnp.float32)
            * score_scale
        )
        same_request = block_requests[:, None] == request[None, :]
        suffix_scores = jnp.where(same_request[None], suffix_scores, -1e30)
        row_max = jnp.maximum(
            jnp.max(prefix_scores, axis=2, keepdims=True),
            jnp.max(suffix_scores, axis=2, keepdims=True),
        )
        prefix_weights = jnp.exp(prefix_scores - row_max)
        suffix_weights = jnp.exp(suffix_scores - row_max)
        denominator = jnp.sum(prefix_weights, axis=2) + jnp.sum(suffix_weights, axis=2)
        weighted = jnp.einsum(
            "hqk,khd->qhd",
            prefix_weights.astype(jnp.bfloat16),
            prefix_values,
            preferred_element_type=jnp.float32,
        )
        weighted = weighted + jnp.einsum(
            "hqk,khd->qhd",
            suffix_weights.astype(jnp.bfloat16),
            value_rows,
            preferred_element_type=jnp.float32,
        )
        return (weighted / jnp.transpose(denominator)[:, :, None]).astype(jnp.bfloat16)

    attended = lax.map(
        block_attend,
        (
            queries.reshape(block_count, block_rows, local_heads, head_dim),
            request.reshape(block_count, block_rows),
        ),
    )
    heads_out = attended.reshape(group_rows, local_width)
    token_heads = lax.all_to_all(
        heads_out.reshape(holders, tok_rows, local_width), "exp", split_axis=0, concat_axis=0,
        tiled=True,
    )
    full_out_weight = lax.all_gather(out_weight, "exp", axis=0, tiled=True)
    attn_sum = jnp.zeros((tok_rows, model_width), jnp.float32)
    for part_index in range(holders):
        partial_sum = jnp.dot(
            token_heads[part_index],
            full_out_weight[part_index * local_width:(part_index + 1) * local_width],
            preferred_element_type=jnp.float32,
        )
        attn_sum = attn_sum + partial_sum.astype(jnp.bfloat16).astype(jnp.float32)
    residual = hidden_f + attn_sum
    normed_moe = rms_scale(residual, norm_moe).astype(jnp.bfloat16)
    req_count = lax.axis_size("req")
    expert_count = req_count * holders // 2
    route_count = routes.shape[1]
    capacity = max(2, tok_rows * route_count * 5 // (4 * expert_count))
    assert capacity % 2 == 0
    slot_total = expert_count * capacity
    slot_of = place_routes(routes, expert_count, capacity)
    slot_hits = (slot_of[:, None] == jnp.arange(slot_total, dtype=jnp.int32)[None, :]).reshape(
        tok_rows, route_count, slot_total
    )
    dispatch = jnp.sum(slot_hits.astype(jnp.int32), axis=1).astype(jnp.bfloat16)
    send_rows = jnp.einsum(
        "ts,td->sd", dispatch, normed_moe, preferred_element_type=jnp.float32
    ).astype(jnp.bfloat16)
    block_shape = aligned_block(capacity // 2 * model_width)
    send_rows = send_rows.reshape((2 * expert_count,) + block_shape)
    arrived = lax.all_to_all(send_rows, ("req", "exp"), split_axis=0, concat_axis=0, tiled=True)
    flat_rows = arrived.reshape(-1, model_width)
    mine = half_apply(flat_rows, expert_gate[0], expert_up[0], expert_down[0])
    other = half_apply(flat_rows, other_gate, other_up, other_down)
    both = (mine.astype(jnp.float32) + other.astype(jnp.float32)).astype(jnp.bfloat16)
    returned = lax.all_to_all(
        both.reshape((2 * expert_count,) + block_shape),
        ("req", "exp"),
        split_axis=0,
        concat_axis=0,
        tiled=True,
    )
    slot_values = returned.reshape(slot_total, model_width).astype(jnp.float32)
    combine = jnp.sum(
        slot_hits.astype(jnp.float32) * route_weights[:, :, None], axis=1
    )
    moe_sum = jnp.dot(
        combine, slot_values, precision=lax.Precision.HIGHEST, preferred_element_type=jnp.float32
    )
    layer_out = (residual + moe_sum).astype(jnp.bfloat16)
    return (
        layer_out,
        key_rows.reshape(group_rows, local_width),
        value_rows.reshape(group_rows, local_width),
    )


def solution(mesh):
    return jax.shard_map(
        on_device,
        mesh=mesh,
        in_specs=(
            P(("req", "exp"), None),
            P(),
            P(None, None, "exp"),
            P("exp", None),
            P("req", "exp", None, None),
            P("req", None),
            P("req", None),
            P(),
            P(("req", "exp"), None),
            P(("req", "exp"), None),
            P(("req", "exp"), None, None),
            P(("req", "exp"), None, None),
            P(("req", "exp"), None, None),
        ),
        out_specs=(P(("req", "exp"), None), P("req", "exp"), P("req", "exp")),
        check_vma=False,
    )
```

```python
import jax
import jax.numpy as jnp
from jax import lax
from jax.sharding import Mesh, PartitionSpec as P

HD = 128
PAGE = 16


eps_norm = 1e-06
rope_base = 10000.0


def rms_scale(inputs, gains_vec):
    return (
        inputs * lax.rsqrt(jnp.mean(inputs * inputs, axis=-1, keepdims=True) + eps_norm) * gains_vec
    )


def positions_of(group_lengths, places, offset):
    end_marks = jnp.cumsum(group_lengths)
    request = jnp.sum((places[:, None] >= end_marks[None, :]).astype(jnp.int32), axis=1)
    starts = end_marks - group_lengths
    onehot = (
        request[:, None] == jnp.arange(group_lengths.shape[0], dtype=jnp.int32)[None, :]
    ).astype(jnp.int32)
    first_place = jnp.sum(onehot * starts[None, :], axis=1)
    return (request, places - first_place + offset)


def rotate(inputs, places):
    half_size = inputs.shape[-1] // 2
    frequency = rope_base ** (-jnp.arange(half_size, dtype=jnp.float32) * 2.0 / inputs.shape[-1])
    angles = places.astype(jnp.float32)[:, None] * frequency[None, :]
    cosine = jnp.cos(angles)[:, None, :]
    sine_part = jnp.sin(angles)[:, None, :]
    lower = inputs[..., :half_size]
    upper = inputs[..., half_size:]
    return jnp.concatenate(
        [lower * cosine - upper * sine_part, upper * cosine + lower * sine_part], axis=-1
    )


def place_routes(block_routes, expert_count, capacity):
    flat_routes = block_routes.reshape(-1)
    entries = flat_routes.shape[0]
    onehot = (flat_routes[:, None] == jnp.arange(expert_count, dtype=jnp.int32)[None, :]).astype(
        jnp.bfloat16
    )
    rows_i = jnp.arange(entries, dtype=jnp.int32)
    earlier = (rows_i[None, :] < rows_i[:, None]).astype(jnp.bfloat16)
    before = jnp.dot(earlier, onehot, preferred_element_type=jnp.float32)
    slot_rank = jnp.sum(before * onehot.astype(jnp.float32), axis=1).astype(jnp.int32)
    return flat_routes * capacity + slot_rank


def aligned_block(size):
    for rows in (16, 8):
        if size % (rows * 128) == 0:
            return (rows, size // rows)
    return (1, size)


def half_apply(flat_rows, gate_mat, up_mat, down_mat):
    gate_proj = jnp.dot(flat_rows, gate_mat, preferred_element_type=jnp.float32)
    up_proj = jnp.dot(flat_rows, up_mat, preferred_element_type=jnp.float32)
    activated = (jax.nn.silu(gate_proj) * up_proj).astype(jnp.bfloat16)
    return jnp.dot(activated, down_mat, preferred_element_type=jnp.float32).astype(jnp.bfloat16)


def on_device(
    hidden,
    norm_attn,
    qkv_weight,
    out_weight,
    prefix_pool,
    page_table,
    suffix_lengths,
    norm_moe,
    routes,
    route_weights,
    expert_gate,
    expert_up,
    expert_down,
):
    tok_rows, model_width = hidden.shape
    chips = lax.axis_size("chip")
    cores = lax.axis_size("core")
    holders = chips * cores
    head_dim = HD
    local_width = qkv_weight.shape[2]
    local_heads = local_width // head_dim
    partner = [(0, 1), (1, 0)]
    other_gate = lax.ppermute(expert_gate[0], "core", partner)
    other_up = lax.ppermute(expert_up[0], "core", partner)
    other_down = lax.ppermute(expert_down[0], "core", partner)
    hidden_f = hidden.astype(jnp.float32)
    normed = rms_scale(hidden_f, norm_attn).astype(jnp.bfloat16)
    group_normed = lax.all_gather(
        lax.all_gather(normed, "chip", axis=0, tiled=True), "core", axis=0, tiled=True
    )
    projected = jnp.einsum(
        "rd,cdh->rch",
        group_normed,
        qkv_weight,
        preferred_element_type=jnp.float32,
    )
    group_rows = projected.shape[0]
    prefix_len = page_table.shape[1] * PAGE
    gathered = jnp.arange(group_rows, dtype=jnp.int32)
    core_of = gathered // (chips * tok_rows)
    chip_of = (gathered // tok_rows) % chips
    token_of = (chip_of * cores + core_of) * tok_rows + gathered % tok_rows
    request, places = positions_of(suffix_lengths[0], token_of, prefix_len)
    projected = projected.reshape(group_rows, 3, local_heads, head_dim)
    queries = rotate(projected[:, 0], places).astype(jnp.bfloat16)
    key_rows = rotate(projected[:, 1], places).astype(jnp.bfloat16)
    value_rows = projected[:, 2].astype(jnp.bfloat16)
    page_rows = page_table[0]
    page_data = lax.all_to_all(
        prefix_pool, ("chip", "core"), split_axis=3, concat_axis=1, tiled=True
    )
    all_slots = jnp.arange(page_data.shape[1], dtype=jnp.int32)
    used_mask = jnp.sum((page_rows[None, :] == all_slots[:, None]).astype(jnp.int32), axis=1) > 0
    prefix_ok = jnp.repeat(used_mask, PAGE)
    page_data = page_data.reshape(-1, local_heads, 2, head_dim)
    prefix_keys = page_data[:, :, 0]
    prefix_values = page_data[:, :, 1]
    score_scale = head_dim ** (-0.5)
    block_rows = min(512, group_rows)
    block_count = group_rows // block_rows

    def block_attend(operands):
        block_queries, block_requests = operands
        prefix_scores = (
            jnp.einsum(
                "qhd,khd->hqk", block_queries, prefix_keys, preferred_element_type=jnp.float32
            )
            * score_scale
        )
        prefix_scores = jnp.where(prefix_ok[None, None, :], prefix_scores, -1e30)
        suffix_scores = (
            jnp.einsum("qhd,khd->hqk", block_queries, key_rows, preferred_element_type=jnp.float32)
            * score_scale
        )
        same_request = block_requests[:, None] == request[None, :]
        suffix_scores = jnp.where(same_request[None], suffix_scores, -1e30)
        row_max = jnp.maximum(
            jnp.max(prefix_scores, axis=2, keepdims=True),
            jnp.max(suffix_scores, axis=2, keepdims=True),
        )
        prefix_weights = jnp.exp(prefix_scores - row_max)
        suffix_weights = jnp.exp(suffix_scores - row_max)
        denominator = jnp.sum(prefix_weights, axis=2) + jnp.sum(suffix_weights, axis=2)
        weighted = jnp.einsum(
            "hqk,khd->qhd",
            prefix_weights.astype(jnp.bfloat16),
            prefix_values,
            preferred_element_type=jnp.float32,
        )
        weighted = weighted + jnp.einsum(
            "hqk,khd->qhd",
            suffix_weights.astype(jnp.bfloat16),
            value_rows,
            preferred_element_type=jnp.float32,
        )
        return (weighted / jnp.transpose(denominator)[:, :, None]).astype(jnp.bfloat16)

    attended = lax.map(
        block_attend,
        (
            queries.reshape(block_count, block_rows, local_heads, head_dim),
            request.reshape(block_count, block_rows),
        ),
    )
    heads_out = attended.reshape(cores, chips, tok_rows, local_width)
    token_heads = lax.all_to_all(
        jnp.transpose(heads_out, (1, 0, 2, 3)).reshape(holders, tok_rows, local_width),
        ("chip", "core"),
        split_axis=0,
        concat_axis=0,
        tiled=True,
    )
    full_out_weight = lax.all_gather(
        lax.all_gather(out_weight, "chip", axis=0, tiled=True), "core", axis=0, tiled=True
    )
    attn_sum = jnp.zeros((tok_rows, model_width), jnp.float32)
    for part_index in range(holders):
        weight_row = (part_index % cores * chips + part_index // cores) * local_width
        partial_sum = jnp.dot(
            token_heads[part_index],
            full_out_weight[weight_row:weight_row + local_width],
            preferred_element_type=jnp.float32,
        )
        attn_sum = attn_sum + partial_sum.astype(jnp.bfloat16).astype(jnp.float32)
    residual = hidden_f + attn_sum
    normed_moe = rms_scale(residual, norm_moe).astype(jnp.bfloat16)
    req_count = lax.axis_size("req")
    expert_count = req_count * holders // 2
    route_count = routes.shape[1]
    capacity = max(2, tok_rows * route_count * 5 // (4 * expert_count))
    assert capacity % 2 == 0
    slot_total = expert_count * capacity
    slot_of = place_routes(routes, expert_count, capacity)
    slot_hits = (slot_of[:, None] == jnp.arange(slot_total, dtype=jnp.int32)[None, :]).reshape(
        tok_rows, route_count, slot_total
    )
    dispatch = jnp.sum(slot_hits.astype(jnp.int32), axis=1).astype(jnp.bfloat16)
    send_rows = jnp.einsum(
        "ts,td->sd", dispatch, normed_moe, preferred_element_type=jnp.float32
    ).astype(jnp.bfloat16)
    block_shape = aligned_block(capacity // 2 * model_width)
    send_rows = send_rows.reshape((2 * expert_count,) + block_shape)
    arrived = lax.all_to_all(
        send_rows, ("req", "chip", "core"), split_axis=0, concat_axis=0, tiled=True
    )
    flat_rows = arrived.reshape(-1, model_width)
    mine = half_apply(flat_rows, expert_gate[0], expert_up[0], expert_down[0])
    other = half_apply(flat_rows, other_gate, other_up, other_down)
    both = (mine.astype(jnp.float32) + other.astype(jnp.float32)).astype(jnp.bfloat16)
    returned = lax.all_to_all(
        both.reshape((2 * expert_count,) + block_shape),
        ("req", "chip", "core"),
        split_axis=0,
        concat_axis=0,
        tiled=True,
    )
    slot_values = returned.reshape(slot_total, model_width).astype(jnp.float32)
    combine = jnp.sum(
        slot_hits.astype(jnp.float32) * route_weights[:, :, None], axis=1
    )
    moe_sum = jnp.dot(
        combine, slot_values, precision=lax.Precision.HIGHEST, preferred_element_type=jnp.float32
    )
    layer_out = (residual + moe_sum).astype(jnp.bfloat16)
    def in_token_order(rows):
        rows = rows.reshape(cores, chips, tok_rows, local_width)
        return jnp.transpose(rows, (1, 0, 2, 3)).reshape(group_rows, local_width)

    return (layer_out, in_token_order(key_rows), in_token_order(value_rows))


def solution(mesh):
    req_size, exp_size = mesh.devices.shape
    pair_mesh = Mesh(mesh.devices.reshape(req_size, exp_size // 2, 2), ("req", "chip", "core"))
    exp = ("chip", "core")
    return jax.shard_map(
        on_device,
        mesh=pair_mesh,
        in_specs=(
            P(("req",) + exp, None),
            P(),
            P(None, None, exp),
            P(exp, None),
            P("req", exp, None, None),
            P("req", None),
            P("req", None),
            P(),
            P(("req",) + exp, None),
            P(("req",) + exp, None),
            P(("req",) + exp, None, None),
            P(("req",) + exp, None, None),
            P(("req",) + exp, None, None),
        ),
        out_specs=(P(("req",) + exp, None), P("req", exp), P("req", exp)),
        check_vma=False,
    )
```

```python
import jax
import jax.numpy as jnp
from jax import lax
from jax.sharding import PartitionSpec as P

HD = 128
PAGE = 16


eps_norm = 1e-06
rope_base = 10000.0


def rms_scale(inputs, gains_vec):
    return (
        inputs * lax.rsqrt(jnp.mean(inputs * inputs, axis=-1, keepdims=True) + eps_norm) * gains_vec
    )


def positions_of(group_lengths, tok_count, offset):
    end_marks = jnp.cumsum(group_lengths)
    places = jnp.arange(tok_count, dtype=jnp.int32)
    request = jnp.sum((places[:, None] >= end_marks[None, :]).astype(jnp.int32), axis=1)
    starts = end_marks - group_lengths
    onehot = (
        request[:, None] == jnp.arange(group_lengths.shape[0], dtype=jnp.int32)[None, :]
    ).astype(jnp.int32)
    first_place = jnp.sum(onehot * starts[None, :], axis=1)
    return (request, places - first_place + offset)


def rotate(inputs, places):
    half_size = inputs.shape[-1] // 2
    frequency = rope_base ** (-jnp.arange(half_size, dtype=jnp.float32) * 2.0 / inputs.shape[-1])
    angles = places.astype(jnp.float32)[:, None] * frequency[None, :]
    cosine = jnp.cos(angles)[:, None, :]
    sine_part = jnp.sin(angles)[:, None, :]
    lower = inputs[..., :half_size]
    upper = inputs[..., half_size:]
    return jnp.concatenate(
        [lower * cosine - upper * sine_part, upper * cosine + lower * sine_part], axis=-1
    )


def place_routes(block_routes, expert_count, capacity):
    flat_routes = block_routes.reshape(-1)
    entries = flat_routes.shape[0]
    onehot = (flat_routes[:, None] == jnp.arange(expert_count, dtype=jnp.int32)[None, :]).astype(
        jnp.bfloat16
    )
    rows_i = jnp.arange(entries, dtype=jnp.int32)
    earlier = (rows_i[None, :] < rows_i[:, None]).astype(jnp.bfloat16)
    before = jnp.dot(earlier, onehot, preferred_element_type=jnp.float32)
    slot_rank = jnp.sum(before * onehot.astype(jnp.float32), axis=1).astype(jnp.int32)
    return flat_routes * capacity + slot_rank


def aligned_block(size):
    for rows in (16, 8):
        if size % (rows * 128) == 0:
            return (rows, size // rows)
    return (1, size)


def half_apply(flat_rows, gate_mat, up_mat, down_mat):
    gate_proj = jnp.dot(flat_rows, gate_mat, preferred_element_type=jnp.float32)
    up_proj = jnp.dot(flat_rows, up_mat, preferred_element_type=jnp.float32)
    activated = (jax.nn.silu(gate_proj) * up_proj).astype(jnp.bfloat16)
    return jnp.dot(activated, down_mat, preferred_element_type=jnp.float32).astype(jnp.bfloat16)


def on_device(
    hidden,
    norm_attn,
    qkv_weight,
    out_weight,
    prefix_pool,
    page_table,
    suffix_lengths,
    norm_moe,
    routes,
    route_weights,
    expert_gate,
    expert_up,
    expert_down,
):
    tok_rows, model_width = hidden.shape
    holders = lax.axis_size("exp")
    head_dim = HD
    local_width = qkv_weight.shape[2]
    local_heads = local_width // head_dim
    partner = [(i, i ^ 1) for i in range(holders)]
    other_gate = lax.ppermute(expert_gate[0], "exp", partner)
    other_up = lax.ppermute(expert_up[0], "exp", partner)
    other_down = lax.ppermute(expert_down[0], "exp", partner)
    hidden_f = hidden.astype(jnp.float32)
    normed = rms_scale(hidden_f, norm_attn).astype(jnp.bfloat16)
    projected = jnp.einsum(
        "rd,cdh->rch",
        lax.all_gather(normed, "exp", axis=0, tiled=True),
        qkv_weight,
        preferred_element_type=jnp.float32,
    )
    group_rows = projected.shape[0]
    prefix_len = page_table.shape[1] * PAGE
    request, places = positions_of(suffix_lengths[0], group_rows, prefix_len)
    projected = projected.reshape(group_rows, 3, local_heads, head_dim)
    queries = rotate(projected[:, 0], places).astype(jnp.bfloat16)
    key_rows = rotate(projected[:, 1], places).astype(jnp.bfloat16)
    value_rows = projected[:, 2].astype(jnp.bfloat16)
    page_rows = page_table[0]
    page_data = lax.all_to_all(prefix_pool, "exp", split_axis=3, concat_axis=1, tiled=True)
    all_slots = jnp.arange(page_data.shape[1], dtype=jnp.int32)
    used_mask = jnp.sum((page_rows[None, :] == all_slots[:, None]).astype(jnp.int32), axis=1) > 0
    prefix_ok = jnp.repeat(used_mask, PAGE)
    page_data = page_data.reshape(-1, local_heads, 2, head_dim)
    prefix_keys = page_data[:, :, 0]
    prefix_values = page_data[:, :, 1]
    score_scale = head_dim ** (-0.5)
    block_rows = min(512, group_rows)
    block_count = group_rows // block_rows

    def block_attend(operands):
        block_queries, block_requests = operands
        prefix_scores = (
            jnp.einsum(
                "qhd,khd->hqk", block_queries, prefix_keys, preferred_element_type=jnp.float32
            )
            * score_scale
        )
        prefix_scores = jnp.where(prefix_ok[None, None, :], prefix_scores, -1e30)
        suffix_scores = (
            jnp.einsum("qhd,khd->hqk", block_queries, key_rows, preferred_element_type=jnp.float32)
            * score_scale
        )
        same_request = block_requests[:, None] == request[None, :]
        suffix_scores = jnp.where(same_request[None], suffix_scores, -1e30)
        row_max = jnp.maximum(
            jnp.max(prefix_scores, axis=2, keepdims=True),
            jnp.max(suffix_scores, axis=2, keepdims=True),
        )
        prefix_weights = jnp.exp(prefix_scores - row_max)
        suffix_weights = jnp.exp(suffix_scores - row_max)
        denominator = jnp.sum(prefix_weights, axis=2) + jnp.sum(suffix_weights, axis=2)
        weighted = jnp.einsum(
            "hqk,khd->qhd",
            prefix_weights.astype(jnp.bfloat16),
            prefix_values,
            preferred_element_type=jnp.float32,
        )
        weighted = weighted + jnp.einsum(
            "hqk,khd->qhd",
            suffix_weights.astype(jnp.bfloat16),
            value_rows,
            preferred_element_type=jnp.float32,
        )
        return (weighted / jnp.transpose(denominator)[:, :, None]).astype(jnp.bfloat16)

    attended = lax.map(
        block_attend,
        (
            queries.reshape(block_count, block_rows, local_heads, head_dim),
            request.reshape(block_count, block_rows),
        ),
    )
    heads_out = attended.reshape(group_rows, local_width)
    token_heads = lax.all_to_all(
        heads_out.reshape(holders, tok_rows, local_width), "exp", split_axis=0, concat_axis=0,
        tiled=True,
    )
    full_out_weight = lax.all_gather(out_weight, "exp", axis=0, tiled=True)
    attn_sum = jnp.zeros((tok_rows, model_width), jnp.float32)
    for part_index in range(holders):
        partial_sum = jnp.dot(
            token_heads[part_index],
            full_out_weight[part_index * local_width:(part_index + 1) * local_width],
            preferred_element_type=jnp.float32,
        )
        attn_sum = attn_sum + partial_sum.astype(jnp.bfloat16).astype(jnp.float32)
    residual = hidden_f + attn_sum
    normed_moe = rms_scale(residual, norm_moe).astype(jnp.bfloat16)
    req_count = lax.axis_size("req")
    expert_count = req_count * holders // 2
    route_count = routes.shape[1]
    capacity = max(2, tok_rows * route_count * 5 // (4 * expert_count))
    assert capacity % 2 == 0
    slot_total = expert_count * capacity
    slot_of = place_routes(routes, expert_count, capacity)
    slot_hits = (slot_of[:, None] == jnp.arange(slot_total, dtype=jnp.int32)[None, :]).reshape(
        tok_rows, route_count, slot_total
    )
    dispatch = jnp.sum(slot_hits.astype(jnp.int32), axis=1).astype(jnp.bfloat16)
    send_rows = jnp.einsum(
        "ts,td->sd", dispatch, normed_moe, preferred_element_type=jnp.float32
    ).astype(jnp.bfloat16)
    chunks = 2 if capacity % 4 == 0 else 1
    chunk_slots = capacity // 2 // chunks
    block_shape = aligned_block(chunk_slots * model_width)
    send_rows = send_rows.reshape(expert_count, 2, chunks, chunk_slots, model_width)
    combine = jnp.sum(
        slot_hits.astype(jnp.float32) * route_weights[:, :, None], axis=1
    ).reshape(tok_rows, expert_count, 2, chunks, chunk_slots)
    moe_sum = jnp.zeros((tok_rows, model_width), jnp.float32)
    for chunk in range(chunks):
        chunk_rows = send_rows[:, :, chunk].reshape((2 * expert_count,) + block_shape)
        arrived = lax.all_to_all(
            chunk_rows, ("req", "exp"), split_axis=0, concat_axis=0, tiled=True
        )
        flat_rows = arrived.reshape(-1, model_width)
        mine = half_apply(flat_rows, expert_gate[0], expert_up[0], expert_down[0])
        other = half_apply(flat_rows, other_gate, other_up, other_down)
        both = (mine.astype(jnp.float32) + other.astype(jnp.float32)).astype(jnp.bfloat16)
        returned = lax.all_to_all(
            both.reshape((2 * expert_count,) + block_shape),
            ("req", "exp"),
            split_axis=0,
            concat_axis=0,
            tiled=True,
        )
        slot_values = returned.reshape(-1, model_width).astype(jnp.float32)
        moe_sum = moe_sum + jnp.dot(
            combine[:, :, :, chunk].reshape(tok_rows, -1),
            slot_values,
            precision=lax.Precision.HIGHEST,
            preferred_element_type=jnp.float32,
        )
    layer_out = (residual + moe_sum).astype(jnp.bfloat16)
    return (
        layer_out,
        key_rows.reshape(group_rows, local_width),
        value_rows.reshape(group_rows, local_width),
    )


def solution(mesh):
    return jax.shard_map(
        on_device,
        mesh=mesh,
        in_specs=(
            P(("req", "exp"), None),
            P(),
            P(None, None, "exp"),
            P("exp", None),
            P("req", "exp", None, None),
            P("req", None),
            P("req", None),
            P(),
            P(("req", "exp"), None),
            P(("req", "exp"), None),
            P(("req", "exp"), None, None),
            P(("req", "exp"), None, None),
            P(("req", "exp"), None, None),
        ),
        out_specs=(P(("req", "exp"), None), P("req", "exp"), P("req", "exp")),
        check_vma=False,
    )
```

```python
import jax
import jax.numpy as jnp
from jax import lax
from jax.sharding import PartitionSpec as P

HD = 128
PAGE = 16


eps_norm = 1e-06
rope_base = 10000.0


def rms_scale(inputs, gains_vec):
    return (
        inputs * lax.rsqrt(jnp.mean(inputs * inputs, axis=-1, keepdims=True) + eps_norm) * gains_vec
    )


def positions_of(group_lengths, tok_count, offset):
    end_marks = jnp.cumsum(group_lengths)
    places = jnp.arange(tok_count, dtype=jnp.int32)
    request = jnp.sum((places[:, None] >= end_marks[None, :]).astype(jnp.int32), axis=1)
    starts = end_marks - group_lengths
    onehot = (
        request[:, None] == jnp.arange(group_lengths.shape[0], dtype=jnp.int32)[None, :]
    ).astype(jnp.int32)
    first_place = jnp.sum(onehot * starts[None, :], axis=1)
    return (request, places - first_place + offset)


def rotate(inputs, places):
    half_size = inputs.shape[-1] // 2
    frequency = rope_base ** (-jnp.arange(half_size, dtype=jnp.float32) * 2.0 / inputs.shape[-1])
    angles = places.astype(jnp.float32)[:, None] * frequency[None, :]
    cosine = jnp.cos(angles)[:, None, :]
    sine_part = jnp.sin(angles)[:, None, :]
    lower = inputs[..., :half_size]
    upper = inputs[..., half_size:]
    return jnp.concatenate(
        [lower * cosine - upper * sine_part, upper * cosine + lower * sine_part], axis=-1
    )


def place_routes(block_routes, expert_count, capacity):
    flat_routes = block_routes.reshape(-1)
    entries = flat_routes.shape[0]
    onehot = (flat_routes[:, None] == jnp.arange(expert_count, dtype=jnp.int32)[None, :]).astype(
        jnp.bfloat16
    )
    rows_i = jnp.arange(entries, dtype=jnp.int32)
    earlier = (rows_i[None, :] < rows_i[:, None]).astype(jnp.bfloat16)
    before = jnp.dot(earlier, onehot, preferred_element_type=jnp.float32)
    slot_rank = jnp.sum(before * onehot.astype(jnp.float32), axis=1).astype(jnp.int32)
    return flat_routes * capacity + slot_rank


def aligned_block(size):
    for rows in (16, 8):
        if size % (rows * 128) == 0:
            return (rows, size // rows)
    return (1, size)


def half_apply(flat_rows, gate_mat, up_mat, down_mat):
    gate_proj = jnp.dot(flat_rows, gate_mat, preferred_element_type=jnp.float32)
    up_proj = jnp.dot(flat_rows, up_mat, preferred_element_type=jnp.float32)
    activated = (jax.nn.silu(gate_proj) * up_proj).astype(jnp.bfloat16)
    return jnp.dot(activated, down_mat, preferred_element_type=jnp.float32).astype(jnp.bfloat16)


def on_device(
    hidden,
    norm_attn,
    qkv_weight,
    out_weight,
    prefix_pool,
    page_table,
    suffix_lengths,
    norm_moe,
    routes,
    route_weights,
    expert_gate,
    expert_up,
    expert_down,
):
    tok_rows, model_width = hidden.shape
    holders = lax.axis_size("exp")
    head_dim = HD
    local_width = qkv_weight.shape[2]
    local_heads = local_width // head_dim
    partner = [(i, i ^ 1) for i in range(holders)]
    other_gate = lax.ppermute(expert_gate[0], "exp", partner)
    other_up = lax.ppermute(expert_up[0], "exp", partner)
    other_down = lax.ppermute(expert_down[0], "exp", partner)
    hidden_f = hidden.astype(jnp.float32)
    normed = rms_scale(hidden_f, norm_attn).astype(jnp.bfloat16)
    projected = jnp.einsum(
        "rd,cdh->rch",
        lax.all_gather(normed, "exp", axis=0, tiled=True),
        qkv_weight,
        preferred_element_type=jnp.float32,
    )
    group_rows = projected.shape[0]
    prefix_len = page_table.shape[1] * PAGE
    request, places = positions_of(suffix_lengths[0], group_rows, prefix_len)
    projected = projected.reshape(group_rows, 3, local_heads, head_dim)
    queries = rotate(projected[:, 0], places).astype(jnp.bfloat16)
    key_rows = rotate(projected[:, 1], places).astype(jnp.bfloat16)
    value_rows = projected[:, 2].astype(jnp.bfloat16)
    page_rows = page_table[0]
    page_data = lax.all_to_all(prefix_pool, "exp", split_axis=3, concat_axis=1, tiled=True)
    all_slots = jnp.arange(page_data.shape[1], dtype=jnp.int32)
    used_mask = jnp.sum((page_rows[None, :] == all_slots[:, None]).astype(jnp.int32), axis=1) > 0
    prefix_ok = jnp.repeat(used_mask, PAGE)
    page_data = page_data.reshape(-1, local_heads, 2, head_dim)
    prefix_keys = page_data[:, :, 0]
    prefix_values = page_data[:, :, 1]
    score_scale = head_dim ** (-0.5)
    block_rows = min(512, group_rows)
    block_count = group_rows // block_rows

    def block_attend(operands):
        block_queries, block_requests = operands
        prefix_scores = (
            jnp.einsum(
                "qhd,khd->hqk", block_queries, prefix_keys, preferred_element_type=jnp.float32
            )
            * score_scale
        )
        prefix_scores = jnp.where(prefix_ok[None, None, :], prefix_scores, -1e30)
        suffix_scores = (
            jnp.einsum("qhd,khd->hqk", block_queries, key_rows, preferred_element_type=jnp.float32)
            * score_scale
        )
        same_request = block_requests[:, None] == request[None, :]
        suffix_scores = jnp.where(same_request[None], suffix_scores, -1e30)
        row_max = jnp.maximum(
            jnp.max(prefix_scores, axis=2, keepdims=True),
            jnp.max(suffix_scores, axis=2, keepdims=True),
        )
        prefix_weights = jnp.exp(prefix_scores - row_max)
        suffix_weights = jnp.exp(suffix_scores - row_max)
        denominator = jnp.sum(prefix_weights, axis=2) + jnp.sum(suffix_weights, axis=2)
        weighted = jnp.einsum(
            "hqk,khd->qhd",
            prefix_weights.astype(jnp.bfloat16),
            prefix_values,
            preferred_element_type=jnp.float32,
        )
        weighted = weighted + jnp.einsum(
            "hqk,khd->qhd",
            suffix_weights.astype(jnp.bfloat16),
            value_rows,
            preferred_element_type=jnp.float32,
        )
        return (weighted / jnp.transpose(denominator)[:, :, None]).astype(jnp.bfloat16)

    attended = lax.map(
        block_attend,
        (
            queries.reshape(block_count, block_rows, local_heads, head_dim),
            request.reshape(block_count, block_rows),
        ),
    )
    heads_out = attended.reshape(group_rows, local_width)
    token_heads = lax.all_to_all(
        heads_out.reshape(holders, tok_rows, local_width), "exp", split_axis=0, concat_axis=0,
        tiled=True,
    )
    full_out_weight = lax.all_gather(out_weight, "exp", axis=0, tiled=True)
    attn_sum = jnp.zeros((tok_rows, model_width), jnp.float32)
    for part_index in range(holders):
        partial_sum = jnp.dot(
            token_heads[part_index],
            full_out_weight[part_index * local_width:(part_index + 1) * local_width],
            preferred_element_type=jnp.float32,
        )
        attn_sum = attn_sum + partial_sum.astype(jnp.bfloat16).astype(jnp.float32)
    residual = hidden_f + attn_sum
    normed_moe = rms_scale(residual, norm_moe).astype(jnp.bfloat16)
    req_count = lax.axis_size("req")
    expert_count = req_count * holders // 2
    route_count = routes.shape[1]
    capacity = max(2, tok_rows * route_count * 5 // (4 * expert_count))
    assert capacity % 2 == 0
    slot_total = expert_count * capacity
    slot_of = place_routes(routes, expert_count, capacity)
    chunks = 2 if capacity % 4 == 0 else 1
    chunk_slots = capacity // 2 // chunks
    chunk_total = 2 * expert_count * chunk_slots
    expert_of, rank_of = slot_of // capacity, slot_of % capacity
    core_of, within = rank_of // (capacity // 2), rank_of % (capacity // 2)
    slot_of = (
        within // chunk_slots * chunk_total
        + (expert_of * 2 + core_of) * chunk_slots
        + within % chunk_slots
    )
    slot_hits = (slot_of[:, None] == jnp.arange(slot_total, dtype=jnp.int32)[None, :]).reshape(
        tok_rows, route_count, slot_total
    )
    dispatch = jnp.sum(slot_hits.astype(jnp.int32), axis=1).astype(jnp.bfloat16)
    send_rows = jnp.einsum(
        "ts,td->sd", dispatch, normed_moe, preferred_element_type=jnp.float32
    ).astype(jnp.bfloat16)
    block_shape = aligned_block(chunk_slots * model_width)
    combine = jnp.sum(slot_hits.astype(jnp.float32) * route_weights[:, :, None], axis=1)
    moe_sum = jnp.zeros((tok_rows, model_width), jnp.float32)
    for chunk in range(chunks):
        chunk_rows = send_rows[chunk * chunk_total:(chunk + 1) * chunk_total]
        chunk_rows = chunk_rows.reshape((2 * expert_count,) + block_shape)
        arrived = lax.all_to_all(
            chunk_rows, ("req", "exp"), split_axis=0, concat_axis=0, tiled=True
        )
        flat_rows = arrived.reshape(-1, model_width)
        mine = half_apply(flat_rows, expert_gate[0], expert_up[0], expert_down[0])
        other = half_apply(flat_rows, other_gate, other_up, other_down)
        both = (mine.astype(jnp.float32) + other.astype(jnp.float32)).astype(jnp.bfloat16)
        returned = lax.all_to_all(
            both.reshape((2 * expert_count,) + block_shape),
            ("req", "exp"),
            split_axis=0,
            concat_axis=0,
            tiled=True,
        )
        slot_values = returned.reshape(-1, model_width).astype(jnp.float32)
        moe_sum = moe_sum + jnp.dot(
            combine[:, chunk * chunk_total:(chunk + 1) * chunk_total],
            slot_values,
            precision=lax.Precision.HIGHEST,
            preferred_element_type=jnp.float32,
        )
    layer_out = (residual + moe_sum).astype(jnp.bfloat16)
    return (
        layer_out,
        key_rows.reshape(group_rows, local_width),
        value_rows.reshape(group_rows, local_width),
    )


def solution(mesh):
    return jax.shard_map(
        on_device,
        mesh=mesh,
        in_specs=(
            P(("req", "exp"), None),
            P(),
            P(None, None, "exp"),
            P("exp", None),
            P("req", "exp", None, None),
            P("req", None),
            P("req", None),
            P(),
            P(("req", "exp"), None),
            P(("req", "exp"), None),
            P(("req", "exp"), None, None),
            P(("req", "exp"), None, None),
            P(("req", "exp"), None, None),
        ),
        out_specs=(P(("req", "exp"), None), P("req", "exp"), P("req", "exp")),
        check_vma=False,
    )
```

```python
import jax
import jax.numpy as jnp
from jax import lax
from jax.sharding import PartitionSpec as P

HD = 128
PAGE = 16


eps_norm = 1e-06
rope_base = 10000.0


def rms_scale(inputs, gains_vec):
    return (
        inputs * lax.rsqrt(jnp.mean(inputs * inputs, axis=-1, keepdims=True) + eps_norm) * gains_vec
    )


def positions_of(group_lengths, tok_count, offset):
    end_marks = jnp.cumsum(group_lengths)
    places = jnp.arange(tok_count, dtype=jnp.int32)
    request = jnp.sum((places[:, None] >= end_marks[None, :]).astype(jnp.int32), axis=1)
    starts = end_marks - group_lengths
    onehot = (
        request[:, None] == jnp.arange(group_lengths.shape[0], dtype=jnp.int32)[None, :]
    ).astype(jnp.int32)
    first_place = jnp.sum(onehot * starts[None, :], axis=1)
    return (request, places - first_place + offset)


def rotate(inputs, places):
    half_size = inputs.shape[-1] // 2
    frequency = rope_base ** (-jnp.arange(half_size, dtype=jnp.float32) * 2.0 / inputs.shape[-1])
    angles = places.astype(jnp.float32)[:, None] * frequency[None, :]
    cosine = jnp.cos(angles)[:, None, :]
    sine_part = jnp.sin(angles)[:, None, :]
    lower = inputs[..., :half_size]
    upper = inputs[..., half_size:]
    return jnp.concatenate(
        [lower * cosine - upper * sine_part, upper * cosine + lower * sine_part], axis=-1
    )


def place_routes(block_routes, expert_count, capacity):
    flat_routes = block_routes.reshape(-1)
    entries = flat_routes.shape[0]
    onehot = (flat_routes[:, None] == jnp.arange(expert_count, dtype=jnp.int32)[None, :]).astype(
        jnp.bfloat16
    )
    rows_i = jnp.arange(entries, dtype=jnp.int32)
    earlier = (rows_i[None, :] < rows_i[:, None]).astype(jnp.bfloat16)
    before = jnp.dot(earlier, onehot, preferred_element_type=jnp.float32)
    slot_rank = jnp.sum(before * onehot.astype(jnp.float32), axis=1).astype(jnp.int32)
    return flat_routes * capacity + slot_rank


def aligned_block(size):
    for rows in (16, 8):
        if size % (rows * 128) == 0:
            return (rows, size // rows)
    return (1, size)


def half_apply(flat_rows, gate_mat, up_mat, down_mat):
    gate_proj = jnp.dot(flat_rows, gate_mat, preferred_element_type=jnp.float32)
    up_proj = jnp.dot(flat_rows, up_mat, preferred_element_type=jnp.float32)
    activated = (jax.nn.silu(gate_proj) * up_proj).astype(jnp.bfloat16)
    return jnp.dot(activated, down_mat, preferred_element_type=jnp.float32).astype(jnp.bfloat16)


def on_device(
    hidden,
    norm_attn,
    qkv_weight,
    out_weight,
    prefix_pool,
    page_table,
    suffix_lengths,
    norm_moe,
    routes,
    route_weights,
    expert_gate,
    expert_up,
    expert_down,
):
    tok_rows, model_width = hidden.shape
    holders = lax.axis_size("exp")
    head_dim = HD
    local_width = qkv_weight.shape[2]
    local_heads = local_width // head_dim
    partner = [(i, i ^ 1) for i in range(holders)]
    other_gate = lax.ppermute(expert_gate[0], "exp", partner)
    other_up = lax.ppermute(expert_up[0], "exp", partner)
    other_down = lax.ppermute(expert_down[0], "exp", partner)
    hidden_f = hidden.astype(jnp.float32)
    normed = rms_scale(hidden_f, norm_attn).astype(jnp.bfloat16)
    projected = jnp.einsum(
        "rd,cdh->rch",
        lax.all_gather(normed, "exp", axis=0, tiled=True),
        qkv_weight,
        preferred_element_type=jnp.float32,
    )
    group_rows = projected.shape[0]
    prefix_len = page_table.shape[1] * PAGE
    request, places = positions_of(suffix_lengths[0], group_rows, prefix_len)
    projected = projected.reshape(group_rows, 3, local_heads, head_dim)
    queries = rotate(projected[:, 0], places).astype(jnp.bfloat16)
    key_rows = rotate(projected[:, 1], places).astype(jnp.bfloat16)
    value_rows = projected[:, 2].astype(jnp.bfloat16)
    page_rows = page_table[0]
    page_data = lax.all_to_all(prefix_pool, "exp", split_axis=3, concat_axis=1, tiled=True)
    page_data = jnp.take(page_data[0], page_rows, axis=0, mode="clip")
    page_data = page_data.reshape(-1, local_heads, 2, head_dim)
    prefix_keys = page_data[:, :, 0]
    prefix_values = page_data[:, :, 1]
    score_scale = head_dim ** (-0.5)
    block_rows = min(512, group_rows)
    block_count = group_rows // block_rows

    def block_attend(operands):
        block_queries, block_requests = operands
        prefix_scores = (
            jnp.einsum(
                "qhd,khd->hqk", block_queries, prefix_keys, preferred_element_type=jnp.float32
            )
            * score_scale
        )
        suffix_scores = (
            jnp.einsum("qhd,khd->hqk", block_queries, key_rows, preferred_element_type=jnp.float32)
            * score_scale
        )
        same_request = block_requests[:, None] == request[None, :]
        suffix_scores = jnp.where(same_request[None], suffix_scores, -1e30)
        row_max = jnp.maximum(
            jnp.max(prefix_scores, axis=2, keepdims=True),
            jnp.max(suffix_scores, axis=2, keepdims=True),
        )
        prefix_weights = jnp.exp(prefix_scores - row_max)
        suffix_weights = jnp.exp(suffix_scores - row_max)
        denominator = jnp.sum(prefix_weights, axis=2) + jnp.sum(suffix_weights, axis=2)
        weighted = jnp.einsum(
            "hqk,khd->qhd",
            prefix_weights.astype(jnp.bfloat16),
            prefix_values,
            preferred_element_type=jnp.float32,
        )
        weighted = weighted + jnp.einsum(
            "hqk,khd->qhd",
            suffix_weights.astype(jnp.bfloat16),
            value_rows,
            preferred_element_type=jnp.float32,
        )
        return (weighted / jnp.transpose(denominator)[:, :, None]).astype(jnp.bfloat16)

    attended = lax.map(
        block_attend,
        (
            queries.reshape(block_count, block_rows, local_heads, head_dim),
            request.reshape(block_count, block_rows),
        ),
    )
    heads_out = attended.reshape(group_rows, local_width)
    token_heads = lax.all_to_all(
        heads_out.reshape(holders, tok_rows, local_width), "exp", split_axis=0, concat_axis=0,
        tiled=True,
    )
    full_out_weight = lax.all_gather(out_weight, "exp", axis=0, tiled=True)
    attn_sum = jnp.zeros((tok_rows, model_width), jnp.float32)
    for part_index in range(holders):
        partial_sum = jnp.dot(
            token_heads[part_index],
            full_out_weight[part_index * local_width:(part_index + 1) * local_width],
            preferred_element_type=jnp.float32,
        )
        attn_sum = attn_sum + partial_sum.astype(jnp.bfloat16).astype(jnp.float32)
    residual = hidden_f + attn_sum
    normed_moe = rms_scale(residual, norm_moe).astype(jnp.bfloat16)
    req_count = lax.axis_size("req")
    expert_count = req_count * holders // 2
    route_count = routes.shape[1]
    capacity = max(2, tok_rows * route_count * 5 // (4 * expert_count))
    assert capacity % 2 == 0
    slot_total = expert_count * capacity
    slot_of = place_routes(routes, expert_count, capacity)
    chunks = 2 if capacity % 4 == 0 else 1
    chunk_slots = capacity // 2 // chunks
    chunk_total = 2 * expert_count * chunk_slots
    expert_of, rank_of = slot_of // capacity, slot_of % capacity
    core_of, within = rank_of // (capacity // 2), rank_of % (capacity // 2)
    slot_of = (
        within // chunk_slots * chunk_total
        + (expert_of * 2 + core_of) * chunk_slots
        + within % chunk_slots
    )
    slot_hits = (slot_of[:, None] == jnp.arange(slot_total, dtype=jnp.int32)[None, :]).reshape(
        tok_rows, route_count, slot_total
    )
    dispatch = jnp.sum(slot_hits.astype(jnp.int32), axis=1).astype(jnp.bfloat16)
    send_rows = jnp.einsum(
        "ts,td->sd", dispatch, normed_moe, preferred_element_type=jnp.float32
    ).astype(jnp.bfloat16)
    block_shape = aligned_block(chunk_slots * model_width)
    combine = jnp.sum(slot_hits.astype(jnp.float32) * route_weights[:, :, None], axis=1)
    hidden_half = expert_gate.shape[2]
    gate_up_mat = jnp.concatenate([expert_gate[0], expert_up[0], other_gate, other_up], axis=1)
    moe_sum = jnp.zeros((tok_rows, model_width), jnp.float32)
    for chunk in range(chunks):
        chunk_rows = send_rows[chunk * chunk_total:(chunk + 1) * chunk_total]
        chunk_rows = chunk_rows.reshape((2 * expert_count,) + block_shape)
        arrived = lax.all_to_all(
            chunk_rows, ("req", "exp"), split_axis=0, concat_axis=0, tiled=True
        )
        flat_rows = arrived.reshape(-1, model_width)
        gate_up = jnp.dot(flat_rows, gate_up_mat, preferred_element_type=jnp.float32)
        gate_up = gate_up.reshape(-1, 2, 2, hidden_half)
        inner = (jax.nn.silu(gate_up[:, :, 0]) * gate_up[:, :, 1]).astype(jnp.bfloat16)
        mine = jnp.dot(inner[:, 0], expert_down[0], preferred_element_type=jnp.float32)
        other = jnp.dot(inner[:, 1], other_down, preferred_element_type=jnp.float32)
        both = (
            mine.astype(jnp.bfloat16).astype(jnp.float32)
            + other.astype(jnp.bfloat16).astype(jnp.float32)
        ).astype(jnp.bfloat16)
        returned = lax.all_to_all(
            both.reshape((2 * expert_count,) + block_shape),
            ("req", "exp"),
            split_axis=0,
            concat_axis=0,
            tiled=True,
        )
        slot_values = returned.reshape(-1, model_width).astype(jnp.float32)
        moe_sum = moe_sum + jnp.dot(
            combine[:, chunk * chunk_total:(chunk + 1) * chunk_total],
            slot_values,
            precision=lax.Precision.HIGHEST,
            preferred_element_type=jnp.float32,
        )
    layer_out = (residual + moe_sum).astype(jnp.bfloat16)
    return (
        layer_out,
        key_rows.reshape(group_rows, local_width),
        value_rows.reshape(group_rows, local_width),
    )


def solution(mesh):
    return jax.shard_map(
        on_device,
        mesh=mesh,
        in_specs=(
            P(("req", "exp"), None),
            P(),
            P(None, None, "exp"),
            P("exp", None),
            P("req", "exp", None, None),
            P("req", None),
            P("req", None),
            P(),
            P(("req", "exp"), None),
            P(("req", "exp"), None),
            P(("req", "exp"), None, None),
            P(("req", "exp"), None, None),
            P(("req", "exp"), None, None),
        ),
        out_specs=(P(("req", "exp"), None), P("req", "exp"), P("req", "exp")),
        check_vma=False,
    )
```

```python
import jax
import jax.numpy as jnp
from jax import lax
from jax.sharding import PartitionSpec as P

HD = 128
PAGE = 16


eps_norm = 1e-06
rope_base = 10000.0


def rms_scale(inputs, gains_vec):
    return (
        inputs * lax.rsqrt(jnp.mean(inputs * inputs, axis=-1, keepdims=True) + eps_norm) * gains_vec
    )


def positions_of(group_lengths, tok_count, offset):
    end_marks = jnp.cumsum(group_lengths)
    places = jnp.arange(tok_count, dtype=jnp.int32)
    request = jnp.sum((places[:, None] >= end_marks[None, :]).astype(jnp.int32), axis=1)
    starts = end_marks - group_lengths
    onehot = (
        request[:, None] == jnp.arange(group_lengths.shape[0], dtype=jnp.int32)[None, :]
    ).astype(jnp.int32)
    first_place = jnp.sum(onehot * starts[None, :], axis=1)
    return (request, places - first_place + offset)


def rotate(inputs, places):
    half_size = inputs.shape[-1] // 2
    frequency = rope_base ** (-jnp.arange(half_size, dtype=jnp.float32) * 2.0 / inputs.shape[-1])
    angles = places.astype(jnp.float32)[:, None] * frequency[None, :]
    cosine = jnp.cos(angles)[:, None, :]
    sine_part = jnp.sin(angles)[:, None, :]
    lower = inputs[..., :half_size]
    upper = inputs[..., half_size:]
    return jnp.concatenate(
        [lower * cosine - upper * sine_part, upper * cosine + lower * sine_part], axis=-1
    )


def place_routes(block_routes, expert_count, capacity):
    flat_routes = block_routes.reshape(-1)
    entries = flat_routes.shape[0]
    onehot = (flat_routes[:, None] == jnp.arange(expert_count, dtype=jnp.int32)[None, :]).astype(
        jnp.bfloat16
    )
    rows_i = jnp.arange(entries, dtype=jnp.int32)
    earlier = (rows_i[None, :] < rows_i[:, None]).astype(jnp.bfloat16)
    before = jnp.dot(earlier, onehot, preferred_element_type=jnp.float32)
    slot_rank = jnp.sum(before * onehot.astype(jnp.float32), axis=1).astype(jnp.int32)
    return flat_routes * capacity + slot_rank


def aligned_block(size):
    for rows in (16, 8):
        if size % (rows * 128) == 0:
            return (rows, size // rows)
    return (1, size)


def half_apply(flat_rows, gate_mat, up_mat, down_mat):
    gate_proj = jnp.dot(flat_rows, gate_mat, preferred_element_type=jnp.float32)
    up_proj = jnp.dot(flat_rows, up_mat, preferred_element_type=jnp.float32)
    activated = (jax.nn.silu(gate_proj) * up_proj).astype(jnp.bfloat16)
    return jnp.dot(activated, down_mat, preferred_element_type=jnp.float32).astype(jnp.bfloat16)


def on_device(
    hidden,
    norm_attn,
    qkv_weight,
    out_weight,
    prefix_pool,
    page_table,
    suffix_lengths,
    norm_moe,
    routes,
    route_weights,
    expert_gate,
    expert_up,
    expert_down,
):
    tok_rows, model_width = hidden.shape
    holders = lax.axis_size("exp")
    head_dim = HD
    local_width = qkv_weight.shape[2]
    local_heads = local_width // head_dim
    partner = [(i, i ^ 1) for i in range(holders)]
    other_gate = lax.ppermute(expert_gate[0], "exp", partner)
    other_up = lax.ppermute(expert_up[0], "exp", partner)
    other_down = lax.ppermute(expert_down[0], "exp", partner)
    core = lax.axis_index("exp") % 2
    half_cols = model_width // 2
    weight_halves = jnp.transpose(out_weight.reshape(local_width, 2, half_cols), (1, 0, 2))
    weight_half = lax.all_to_all(
        jnp.broadcast_to(weight_halves[None], (holders // 2, 2, local_width, half_cols)).reshape(
            holders, local_width, half_cols
        ),
        "exp",
        split_axis=0,
        concat_axis=0,
        tiled=True,
    )
    hidden_f = hidden.astype(jnp.float32)
    normed = rms_scale(hidden_f, norm_attn).astype(jnp.bfloat16)
    projected = jnp.einsum(
        "rd,cdh->rch",
        lax.all_gather(normed, "exp", axis=0, tiled=True),
        qkv_weight,
        preferred_element_type=jnp.float32,
    )
    group_rows = projected.shape[0]
    prefix_len = page_table.shape[1] * PAGE
    request, places = positions_of(suffix_lengths[0], group_rows, prefix_len)
    projected = projected.reshape(group_rows, 3, local_heads, head_dim)
    queries = rotate(projected[:, 0], places).astype(jnp.bfloat16)
    key_rows = rotate(projected[:, 1], places).astype(jnp.bfloat16)
    value_rows = projected[:, 2].astype(jnp.bfloat16)
    page_rows = page_table[0]
    page_data = lax.all_to_all(prefix_pool, "exp", split_axis=3, concat_axis=1, tiled=True)
    page_data = jnp.take(page_data[0], page_rows, axis=0, mode="clip")
    page_data = page_data.reshape(-1, local_heads, 2, head_dim)
    prefix_keys = page_data[:, :, 0]
    prefix_values = page_data[:, :, 1]
    score_scale = head_dim ** (-0.5)
    block_rows = min(512, group_rows)
    block_count = group_rows // block_rows

    def block_attend(operands):
        block_queries, block_requests = operands
        prefix_scores = (
            jnp.einsum(
                "qhd,khd->hqk", block_queries, prefix_keys, preferred_element_type=jnp.float32
            )
            * score_scale
        )
        suffix_scores = (
            jnp.einsum("qhd,khd->hqk", block_queries, key_rows, preferred_element_type=jnp.float32)
            * score_scale
        )
        same_request = block_requests[:, None] == request[None, :]
        suffix_scores = jnp.where(same_request[None], suffix_scores, -1e30)
        row_max = jnp.maximum(
            jnp.max(prefix_scores, axis=2, keepdims=True),
            jnp.max(suffix_scores, axis=2, keepdims=True),
        )
        prefix_weights = jnp.exp(prefix_scores - row_max)
        suffix_weights = jnp.exp(suffix_scores - row_max)
        denominator = jnp.sum(prefix_weights, axis=2) + jnp.sum(suffix_weights, axis=2)
        weighted = jnp.einsum(
            "hqk,khd->qhd",
            prefix_weights.astype(jnp.bfloat16),
            prefix_values,
            preferred_element_type=jnp.float32,
        )
        weighted = weighted + jnp.einsum(
            "hqk,khd->qhd",
            suffix_weights.astype(jnp.bfloat16),
            value_rows,
            preferred_element_type=jnp.float32,
        )
        return (weighted / jnp.transpose(denominator)[:, :, None]).astype(jnp.bfloat16)

    attended = lax.map(
        block_attend,
        (
            queries.reshape(block_count, block_rows, local_heads, head_dim),
            request.reshape(block_count, block_rows),
        ),
    )
    heads_out = attended.reshape(group_rows, local_width)
    chip_rows = 2 * tok_rows
    token_heads = lax.all_to_all(
        jnp.broadcast_to(
            heads_out.reshape(holders // 2, 1, chip_rows, local_width),
            (holders // 2, 2, chip_rows, local_width),
        ).reshape(holders, chip_rows, local_width),
        "exp",
        split_axis=0,
        concat_axis=0,
        tiled=True,
    )
    attn_half = jnp.zeros((chip_rows, half_cols), jnp.float32)
    for part_index in range(holders):
        partial_sum = jnp.dot(
            token_heads[part_index], weight_half[part_index], preferred_element_type=jnp.float32
        )
        attn_half = attn_half + partial_sum.astype(jnp.bfloat16).astype(jnp.float32)
    keep_part = lax.dynamic_slice_in_dim(attn_half, core * tok_rows, tok_rows, 0)
    send_part = lax.dynamic_slice_in_dim(attn_half, (1 - core) * tok_rows, tok_rows, 0)
    got_part = lax.ppermute(send_part, "exp", partner)
    attn_sum = jnp.where(
        core == 0,
        jnp.concatenate([keep_part, got_part], axis=1),
        jnp.concatenate([got_part, keep_part], axis=1),
    )
    residual = hidden_f + attn_sum
    normed_moe = rms_scale(residual, norm_moe).astype(jnp.bfloat16)
    req_count = lax.axis_size("req")
    expert_count = req_count * holders // 2
    route_count = routes.shape[1]
    capacity = max(2, tok_rows * route_count * 5 // (4 * expert_count))
    assert capacity % 2 == 0
    slot_total = expert_count * capacity
    slot_of = place_routes(routes, expert_count, capacity)
    chunks = 2 if capacity % 4 == 0 else 1
    chunk_slots = capacity // 2 // chunks
    chunk_total = 2 * expert_count * chunk_slots
    expert_of, rank_of = slot_of // capacity, slot_of % capacity
    core_of, within = rank_of // (capacity // 2), rank_of % (capacity // 2)
    slot_of = (
        within // chunk_slots * chunk_total
        + (expert_of * 2 + core_of) * chunk_slots
        + within % chunk_slots
    )
    slot_hits = (slot_of[:, None] == jnp.arange(slot_total, dtype=jnp.int32)[None, :]).reshape(
        tok_rows, route_count, slot_total
    )
    dispatch = jnp.sum(slot_hits.astype(jnp.int32), axis=1).astype(jnp.bfloat16)
    send_rows = jnp.einsum(
        "ts,td->sd", dispatch, normed_moe, preferred_element_type=jnp.float32
    ).astype(jnp.bfloat16)
    block_shape = aligned_block(chunk_slots * model_width)
    combine = jnp.sum(slot_hits.astype(jnp.float32) * route_weights[:, :, None], axis=1)
    hidden_half = expert_gate.shape[2]
    gate_up_mat = jnp.concatenate([expert_gate[0], expert_up[0], other_gate, other_up], axis=1)
    moe_sum = jnp.zeros((tok_rows, model_width), jnp.float32)
    for chunk in range(chunks):
        chunk_rows = send_rows[chunk * chunk_total:(chunk + 1) * chunk_total]
        chunk_rows = chunk_rows.reshape((2 * expert_count,) + block_shape)
        arrived = lax.all_to_all(
            chunk_rows, ("req", "exp"), split_axis=0, concat_axis=0, tiled=True
        )
        flat_rows = arrived.reshape(-1, model_width)
        gate_up = jnp.dot(flat_rows, gate_up_mat, preferred_element_type=jnp.float32)
        gate_up = gate_up.reshape(-1, 2, 2, hidden_half)
        inner = (jax.nn.silu(gate_up[:, :, 0]) * gate_up[:, :, 1]).astype(jnp.bfloat16)
        mine = jnp.dot(inner[:, 0], expert_down[0], preferred_element_type=jnp.float32)
        other = jnp.dot(inner[:, 1], other_down, preferred_element_type=jnp.float32)
        both = (
            mine.astype(jnp.bfloat16).astype(jnp.float32)
            + other.astype(jnp.bfloat16).astype(jnp.float32)
        ).astype(jnp.bfloat16)
        returned = lax.all_to_all(
            both.reshape((2 * expert_count,) + block_shape),
            ("req", "exp"),
            split_axis=0,
            concat_axis=0,
            tiled=True,
        )
        slot_values = returned.reshape(-1, model_width).astype(jnp.float32)
        moe_sum = moe_sum + jnp.dot(
            combine[:, chunk * chunk_total:(chunk + 1) * chunk_total],
            slot_values,
            precision=lax.Precision.HIGHEST,
            preferred_element_type=jnp.float32,
        )
    layer_out = (residual + moe_sum).astype(jnp.bfloat16)
    return (
        layer_out,
        key_rows.reshape(group_rows, local_width),
        value_rows.reshape(group_rows, local_width),
    )


def solution(mesh):
    return jax.shard_map(
        on_device,
        mesh=mesh,
        in_specs=(
            P(("req", "exp"), None),
            P(),
            P(None, None, "exp"),
            P("exp", None),
            P("req", "exp", None, None),
            P("req", None),
            P("req", None),
            P(),
            P(("req", "exp"), None),
            P(("req", "exp"), None),
            P(("req", "exp"), None, None),
            P(("req", "exp"), None, None),
            P(("req", "exp"), None, None),
        ),
        out_specs=(P(("req", "exp"), None), P("req", "exp"), P("req", "exp")),
        check_vma=False,
    )
```

```python
import jax
import jax.numpy as jnp
from jax import lax
from jax.sharding import PartitionSpec as P

HD = 128
PAGE = 16


eps_norm = 1e-06
rope_base = 10000.0


def rms_scale(inputs, gains_vec):
    return (
        inputs * lax.rsqrt(jnp.mean(inputs * inputs, axis=-1, keepdims=True) + eps_norm) * gains_vec
    )


def positions_of(group_lengths, tok_count, offset):
    end_marks = jnp.cumsum(group_lengths)
    places = jnp.arange(tok_count, dtype=jnp.int32)
    request = jnp.sum((places[:, None] >= end_marks[None, :]).astype(jnp.int32), axis=1)
    starts = end_marks - group_lengths
    onehot = (
        request[:, None] == jnp.arange(group_lengths.shape[0], dtype=jnp.int32)[None, :]
    ).astype(jnp.int32)
    first_place = jnp.sum(onehot * starts[None, :], axis=1)
    return (request, places - first_place + offset)


def rotate(inputs, places):
    half_size = inputs.shape[-1] // 2
    frequency = rope_base ** (-jnp.arange(half_size, dtype=jnp.float32) * 2.0 / inputs.shape[-1])
    angles = places.astype(jnp.float32)[:, None] * frequency[None, :]
    cosine = jnp.cos(angles)[:, None, :]
    sine_part = jnp.sin(angles)[:, None, :]
    lower = inputs[..., :half_size]
    upper = inputs[..., half_size:]
    return jnp.concatenate(
        [lower * cosine - upper * sine_part, upper * cosine + lower * sine_part], axis=-1
    )


def place_routes(block_routes, expert_count, capacity):
    flat_routes = block_routes.reshape(-1)
    entries = flat_routes.shape[0]
    onehot = (flat_routes[:, None] == jnp.arange(expert_count, dtype=jnp.int32)[None, :]).astype(
        jnp.bfloat16
    )
    rows_i = jnp.arange(entries, dtype=jnp.int32)
    earlier = (rows_i[None, :] < rows_i[:, None]).astype(jnp.bfloat16)
    before = jnp.dot(earlier, onehot, preferred_element_type=jnp.float32)
    slot_rank = jnp.sum(before * onehot.astype(jnp.float32), axis=1).astype(jnp.int32)
    return flat_routes * capacity + slot_rank


def aligned_block(size):
    for rows in (16, 8):
        if size % (rows * 128) == 0:
            return (rows, size // rows)
    return (1, size)


def half_apply(flat_rows, gate_mat, up_mat, down_mat):
    gate_proj = jnp.dot(flat_rows, gate_mat, preferred_element_type=jnp.float32)
    up_proj = jnp.dot(flat_rows, up_mat, preferred_element_type=jnp.float32)
    activated = (jax.nn.silu(gate_proj) * up_proj).astype(jnp.bfloat16)
    return jnp.dot(activated, down_mat, preferred_element_type=jnp.float32).astype(jnp.bfloat16)


def on_device(
    hidden,
    norm_attn,
    qkv_weight,
    out_weight,
    prefix_pool,
    page_table,
    suffix_lengths,
    norm_moe,
    routes,
    route_weights,
    expert_gate,
    expert_up,
    expert_down,
):
    tok_rows, model_width = hidden.shape
    holders = lax.axis_size("exp")
    head_dim = HD
    local_width = qkv_weight.shape[2]
    local_heads = local_width // head_dim
    partner = [(i, i ^ 1) for i in range(holders)]
    other_gate = lax.ppermute(expert_gate[0], "exp", partner)
    other_up = lax.ppermute(expert_up[0], "exp", partner)
    other_down = lax.ppermute(expert_down[0], "exp", partner)
    second_cols = lax.all_to_all(
        jnp.broadcast_to(
            out_weight[None, :, model_width // 2:], (holders,) + (local_width, model_width // 2)
        ),
        "exp",
        split_axis=0,
        concat_axis=0,
        tiled=True,
    )
    hidden_f = hidden.astype(jnp.float32)
    normed = rms_scale(hidden_f, norm_attn).astype(jnp.bfloat16)
    projected = jnp.einsum(
        "rd,cdh->rch",
        lax.all_gather(normed, "exp", axis=0, tiled=True),
        qkv_weight,
        preferred_element_type=jnp.float32,
    )
    group_rows = projected.shape[0]
    prefix_len = page_table.shape[1] * PAGE
    request, places = positions_of(suffix_lengths[0], group_rows, prefix_len)
    projected = projected.reshape(group_rows, 3, local_heads, head_dim)
    queries = rotate(projected[:, 0], places).astype(jnp.bfloat16)
    key_rows = rotate(projected[:, 1], places).astype(jnp.bfloat16)
    value_rows = projected[:, 2].astype(jnp.bfloat16)
    page_rows = page_table[0]
    page_data = lax.all_to_all(prefix_pool, "exp", split_axis=3, concat_axis=1, tiled=True)
    page_data = jnp.take(page_data[0], page_rows, axis=0, mode="clip")
    second_cols, page_data = lax.optimization_barrier((second_cols, page_data))
    page_data = page_data.reshape(-1, local_heads, 2, head_dim)
    prefix_keys = page_data[:, :, 0]
    prefix_values = page_data[:, :, 1]
    score_scale = head_dim ** (-0.5)
    block_rows = min(512, group_rows)
    block_count = group_rows // block_rows

    def block_attend(operands):
        block_queries, block_requests = operands
        prefix_scores = (
            jnp.einsum(
                "qhd,khd->hqk", block_queries, prefix_keys, preferred_element_type=jnp.float32
            )
            * score_scale
        )
        suffix_scores = (
            jnp.einsum("qhd,khd->hqk", block_queries, key_rows, preferred_element_type=jnp.float32)
            * score_scale
        )
        same_request = block_requests[:, None] == request[None, :]
        suffix_scores = jnp.where(same_request[None], suffix_scores, -1e30)
        row_max = jnp.maximum(
            jnp.max(prefix_scores, axis=2, keepdims=True),
            jnp.max(suffix_scores, axis=2, keepdims=True),
        )
        prefix_weights = jnp.exp(prefix_scores - row_max)
        suffix_weights = jnp.exp(suffix_scores - row_max)
        denominator = jnp.sum(prefix_weights, axis=2) + jnp.sum(suffix_weights, axis=2)
        weighted = jnp.einsum(
            "hqk,khd->qhd",
            prefix_weights.astype(jnp.bfloat16),
            prefix_values,
            preferred_element_type=jnp.float32,
        )
        weighted = weighted + jnp.einsum(
            "hqk,khd->qhd",
            suffix_weights.astype(jnp.bfloat16),
            value_rows,
            preferred_element_type=jnp.float32,
        )
        return (weighted / jnp.transpose(denominator)[:, :, None]).astype(jnp.bfloat16)

    attended = lax.map(
        block_attend,
        (
            queries.reshape(block_count, block_rows, local_heads, head_dim),
            request.reshape(block_count, block_rows),
        ),
    )
    heads_out = attended.reshape(group_rows, local_width)
    token_heads = lax.all_to_all(
        heads_out.reshape(holders, tok_rows, local_width), "exp", split_axis=0, concat_axis=0,
        tiled=True,
    )
    half_cols = model_width // 2
    first_cols = lax.all_gather(out_weight[:, :half_cols], "exp", axis=0, tiled=True)
    first_cols = first_cols.reshape(holders, local_width, half_cols)
    column_parts = []
    for weight_part in (first_cols, second_cols):
        attn_part = jnp.zeros((tok_rows, half_cols), jnp.float32)
        for part_index in range(holders):
            partial_sum = jnp.dot(
                token_heads[part_index], weight_part[part_index],
                preferred_element_type=jnp.float32,
            )
            attn_part = attn_part + partial_sum.astype(jnp.bfloat16).astype(jnp.float32)
        column_parts.append(attn_part)
    residual = hidden_f + jnp.concatenate(column_parts, axis=1)
    normed_moe = rms_scale(residual, norm_moe).astype(jnp.bfloat16)
    req_count = lax.axis_size("req")
    expert_count = req_count * holders // 2
    route_count = routes.shape[1]
    capacity = max(2, tok_rows * route_count * 5 // (4 * expert_count))
    assert capacity % 2 == 0
    slot_total = expert_count * capacity
    slot_of = place_routes(routes, expert_count, capacity)
    chunks = 2 if capacity % 4 == 0 else 1
    chunk_slots = capacity // 2 // chunks
    chunk_total = 2 * expert_count * chunk_slots
    expert_of, rank_of = slot_of // capacity, slot_of % capacity
    core_of, within = rank_of // (capacity // 2), rank_of % (capacity // 2)
    slot_of = (
        within // chunk_slots * chunk_total
        + (expert_of * 2 + core_of) * chunk_slots
        + within % chunk_slots
    )
    slot_hits = (slot_of[:, None] == jnp.arange(slot_total, dtype=jnp.int32)[None, :]).reshape(
        tok_rows, route_count, slot_total
    )
    dispatch = jnp.sum(slot_hits.astype(jnp.int32), axis=1).astype(jnp.bfloat16)
    send_rows = jnp.einsum(
        "ts,td->sd", dispatch, normed_moe, preferred_element_type=jnp.float32
    ).astype(jnp.bfloat16)
    block_shape = aligned_block(chunk_slots * model_width)
    combine = jnp.sum(slot_hits.astype(jnp.float32) * route_weights[:, :, None], axis=1)
    hidden_half = expert_gate.shape[2]
    gate_up_mat = jnp.concatenate([expert_gate[0], expert_up[0], other_gate, other_up], axis=1)
    moe_sum = jnp.zeros((tok_rows, model_width), jnp.float32)
    for chunk in range(chunks):
        chunk_rows = send_rows[chunk * chunk_total:(chunk + 1) * chunk_total]
        chunk_rows = chunk_rows.reshape((2 * expert_count,) + block_shape)
        arrived = lax.all_to_all(
            chunk_rows, ("req", "exp"), split_axis=0, concat_axis=0, tiled=True
        )
        flat_rows = arrived.reshape(-1, model_width)
        gate_up = jnp.dot(flat_rows, gate_up_mat, preferred_element_type=jnp.float32)
        gate_up = gate_up.reshape(-1, 2, 2, hidden_half)
        inner = (jax.nn.silu(gate_up[:, :, 0]) * gate_up[:, :, 1]).astype(jnp.bfloat16)
        mine = jnp.dot(inner[:, 0], expert_down[0], preferred_element_type=jnp.float32)
        other = jnp.dot(inner[:, 1], other_down, preferred_element_type=jnp.float32)
        both = (
            mine.astype(jnp.bfloat16).astype(jnp.float32)
            + other.astype(jnp.bfloat16).astype(jnp.float32)
        ).astype(jnp.bfloat16)
        returned = lax.all_to_all(
            both.reshape((2 * expert_count,) + block_shape),
            ("req", "exp"),
            split_axis=0,
            concat_axis=0,
            tiled=True,
        )
        slot_values = returned.reshape(-1, model_width).astype(jnp.float32)
        moe_sum = moe_sum + jnp.dot(
            combine[:, chunk * chunk_total:(chunk + 1) * chunk_total],
            slot_values,
            precision=lax.Precision.HIGHEST,
            preferred_element_type=jnp.float32,
        )
    layer_out = (residual + moe_sum).astype(jnp.bfloat16)
    return (
        layer_out,
        key_rows.reshape(group_rows, local_width),
        value_rows.reshape(group_rows, local_width),
    )


def solution(mesh):
    return jax.shard_map(
        on_device,
        mesh=mesh,
        in_specs=(
            P(("req", "exp"), None),
            P(),
            P(None, None, "exp"),
            P("exp", None),
            P("req", "exp", None, None),
            P("req", None),
            P("req", None),
            P(),
            P(("req", "exp"), None),
            P(("req", "exp"), None),
            P(("req", "exp"), None, None),
            P(("req", "exp"), None, None),
            P(("req", "exp"), None, None),
        ),
        out_specs=(P(("req", "exp"), None), P("req", "exp"), P("req", "exp")),
        check_vma=False,
    )
```

```python
import jax
import jax.numpy as jnp
from jax import lax
from jax.sharding import PartitionSpec as P

HD = 128
PAGE = 16


eps_norm = 1e-06
rope_base = 10000.0


def rms_scale(inputs, gains_vec):
    return (
        inputs * lax.rsqrt(jnp.mean(inputs * inputs, axis=-1, keepdims=True) + eps_norm) * gains_vec
    )


def positions_of(group_lengths, tok_count, offset):
    end_marks = jnp.cumsum(group_lengths)
    places = jnp.arange(tok_count, dtype=jnp.int32)
    request = jnp.sum((places[:, None] >= end_marks[None, :]).astype(jnp.int32), axis=1)
    starts = end_marks - group_lengths
    onehot = (
        request[:, None] == jnp.arange(group_lengths.shape[0], dtype=jnp.int32)[None, :]
    ).astype(jnp.int32)
    first_place = jnp.sum(onehot * starts[None, :], axis=1)
    return (request, places - first_place + offset)


def rotate(inputs, places):
    half_size = inputs.shape[-1] // 2
    frequency = rope_base ** (-jnp.arange(half_size, dtype=jnp.float32) * 2.0 / inputs.shape[-1])
    angles = places.astype(jnp.float32)[:, None] * frequency[None, :]
    cosine = jnp.cos(angles)[:, None, :]
    sine_part = jnp.sin(angles)[:, None, :]
    lower = inputs[..., :half_size]
    upper = inputs[..., half_size:]
    return jnp.concatenate(
        [lower * cosine - upper * sine_part, upper * cosine + lower * sine_part], axis=-1
    )


def place_routes(block_routes, expert_count, capacity):
    flat_routes = block_routes.reshape(-1)
    entries = flat_routes.shape[0]
    onehot = (flat_routes[:, None] == jnp.arange(expert_count, dtype=jnp.int32)[None, :]).astype(
        jnp.bfloat16
    )
    rows_i = jnp.arange(entries, dtype=jnp.int32)
    earlier = (rows_i[None, :] < rows_i[:, None]).astype(jnp.bfloat16)
    before = jnp.dot(earlier, onehot, preferred_element_type=jnp.float32)
    slot_rank = jnp.sum(before * onehot.astype(jnp.float32), axis=1).astype(jnp.int32)
    return flat_routes * capacity + slot_rank


def aligned_block(size):
    for rows in (16, 8):
        if size % (rows * 128) == 0:
            return (rows, size // rows)
    return (1, size)


def half_apply(flat_rows, gate_mat, up_mat, down_mat):
    gate_proj = jnp.dot(flat_rows, gate_mat, preferred_element_type=jnp.float32)
    up_proj = jnp.dot(flat_rows, up_mat, preferred_element_type=jnp.float32)
    activated = (jax.nn.silu(gate_proj) * up_proj).astype(jnp.bfloat16)
    return jnp.dot(activated, down_mat, preferred_element_type=jnp.float32).astype(jnp.bfloat16)


def on_device(
    hidden,
    norm_attn,
    qkv_weight,
    out_weight,
    prefix_pool,
    page_table,
    suffix_lengths,
    norm_moe,
    routes,
    route_weights,
    expert_gate,
    expert_up,
    expert_down,
):
    tok_rows, model_width = hidden.shape
    holders = lax.axis_size("exp")
    head_dim = HD
    local_width = qkv_weight.shape[2]
    local_heads = local_width // head_dim
    partner = [(i, i ^ 1) for i in range(holders)]
    other_gate = lax.ppermute(expert_gate[0], "exp", partner)
    other_up = lax.ppermute(expert_up[0], "exp", partner)
    other_down = lax.ppermute(expert_down[0], "exp", partner)
    hidden_f = hidden.astype(jnp.float32)
    normed = rms_scale(hidden_f, norm_attn).astype(jnp.bfloat16)
    projected = jnp.einsum(
        "rd,cdh->rch",
        lax.all_gather(normed, "exp", axis=0, tiled=True),
        qkv_weight,
        preferred_element_type=jnp.float32,
    )
    group_rows = projected.shape[0]
    prefix_len = page_table.shape[1] * PAGE
    request, places = positions_of(suffix_lengths[0], group_rows, prefix_len)
    projected = projected.reshape(group_rows, 3, local_heads, head_dim)
    queries = rotate(projected[:, 0], places).astype(jnp.bfloat16)
    key_rows = rotate(projected[:, 1], places).astype(jnp.bfloat16)
    value_rows = projected[:, 2].astype(jnp.bfloat16)
    page_rows = page_table[0]
    own_pages = prefix_pool.shape[1]
    own_first = lax.axis_index("exp") * own_pages
    named = jnp.any(
        page_rows[None, :] == own_first + jnp.arange(own_pages, dtype=jnp.int32)[:, None],
        axis=1,
    )
    order = jnp.argsort(jnp.where(named, 0, 1).astype(jnp.int32), stable=True)
    named_pages = jnp.take(prefix_pool[0], order[: own_pages // 2], axis=0, mode="clip")
    page_data = lax.all_to_all(named_pages, "exp", split_axis=2, concat_axis=0, tiled=True)
    page_data = page_data.reshape(-1, local_heads, 2, head_dim)
    prefix_keys = page_data[:, :, 0]
    prefix_values = page_data[:, :, 1]
    score_scale = head_dim ** (-0.5)
    block_rows = min(512, group_rows)
    block_count = group_rows // block_rows

    def block_attend(operands):
        block_queries, block_requests = operands
        prefix_scores = (
            jnp.einsum(
                "qhd,khd->hqk", block_queries, prefix_keys, preferred_element_type=jnp.float32
            )
            * score_scale
        )
        suffix_scores = (
            jnp.einsum("qhd,khd->hqk", block_queries, key_rows, preferred_element_type=jnp.float32)
            * score_scale
        )
        same_request = block_requests[:, None] == request[None, :]
        suffix_scores = jnp.where(same_request[None], suffix_scores, -1e30)
        row_max = jnp.maximum(
            jnp.max(prefix_scores, axis=2, keepdims=True),
            jnp.max(suffix_scores, axis=2, keepdims=True),
        )
        prefix_weights = jnp.exp(prefix_scores - row_max)
        suffix_weights = jnp.exp(suffix_scores - row_max)
        denominator = jnp.sum(prefix_weights, axis=2) + jnp.sum(suffix_weights, axis=2)
        weighted = jnp.einsum(
            "hqk,khd->qhd",
            prefix_weights.astype(jnp.bfloat16),
            prefix_values,
            preferred_element_type=jnp.float32,
        )
        weighted = weighted + jnp.einsum(
            "hqk,khd->qhd",
            suffix_weights.astype(jnp.bfloat16),
            value_rows,
            preferred_element_type=jnp.float32,
        )
        return (weighted / jnp.transpose(denominator)[:, :, None]).astype(jnp.bfloat16)

    attended = lax.map(
        block_attend,
        (
            queries.reshape(block_count, block_rows, local_heads, head_dim),
            request.reshape(block_count, block_rows),
        ),
    )
    heads_out = attended.reshape(group_rows, local_width)
    token_heads = lax.all_to_all(
        heads_out.reshape(holders, tok_rows, local_width), "exp", split_axis=0, concat_axis=0,
        tiled=True,
    )
    full_out_weight = lax.all_gather(out_weight, "exp", axis=0, tiled=True)
    attn_sum = jnp.zeros((tok_rows, model_width), jnp.float32)
    for part_index in range(holders):
        partial_sum = jnp.dot(
            token_heads[part_index],
            full_out_weight[part_index * local_width:(part_index + 1) * local_width],
            preferred_element_type=jnp.float32,
        )
        attn_sum = attn_sum + partial_sum.astype(jnp.bfloat16).astype(jnp.float32)
    residual = hidden_f + attn_sum
    normed_moe = rms_scale(residual, norm_moe).astype(jnp.bfloat16)
    req_count = lax.axis_size("req")
    expert_count = req_count * holders // 2
    route_count = routes.shape[1]
    capacity = max(2, tok_rows * route_count * 5 // (4 * expert_count))
    assert capacity % 2 == 0
    slot_total = expert_count * capacity
    slot_of = place_routes(routes, expert_count, capacity)
    chunks = 2 if capacity % 4 == 0 else 1
    chunk_slots = capacity // 2 // chunks
    chunk_total = 2 * expert_count * chunk_slots
    expert_of, rank_of = slot_of // capacity, slot_of % capacity
    core_of, within = rank_of // (capacity // 2), rank_of % (capacity // 2)
    slot_of = (
        within // chunk_slots * chunk_total
        + (expert_of * 2 + core_of) * chunk_slots
        + within % chunk_slots
    )
    slot_hits = (slot_of[:, None] == jnp.arange(slot_total, dtype=jnp.int32)[None, :]).reshape(
        tok_rows, route_count, slot_total
    )
    dispatch = jnp.sum(slot_hits.astype(jnp.int32), axis=1).astype(jnp.bfloat16)
    send_rows = jnp.einsum(
        "ts,td->sd", dispatch, normed_moe, preferred_element_type=jnp.float32
    ).astype(jnp.bfloat16)
    block_shape = aligned_block(chunk_slots * model_width)
    combine = jnp.sum(slot_hits.astype(jnp.float32) * route_weights[:, :, None], axis=1)
    hidden_half = expert_gate.shape[2]
    gate_up_mat = jnp.concatenate([expert_gate[0], expert_up[0], other_gate, other_up], axis=1)
    moe_sum = jnp.zeros((tok_rows, model_width), jnp.float32)
    for chunk in range(chunks):
        chunk_rows = send_rows[chunk * chunk_total:(chunk + 1) * chunk_total]
        chunk_rows = chunk_rows.reshape((2 * expert_count,) + block_shape)
        arrived = lax.all_to_all(
            chunk_rows, ("req", "exp"), split_axis=0, concat_axis=0, tiled=True
        )
        flat_rows = arrived.reshape(-1, model_width)
        gate_up = jnp.dot(flat_rows, gate_up_mat, preferred_element_type=jnp.float32)
        gate_up = gate_up.reshape(-1, 2, 2, hidden_half)
        inner = (jax.nn.silu(gate_up[:, :, 0]) * gate_up[:, :, 1]).astype(jnp.bfloat16)
        mine = jnp.dot(inner[:, 0], expert_down[0], preferred_element_type=jnp.float32)
        other = jnp.dot(inner[:, 1], other_down, preferred_element_type=jnp.float32)
        both = (
            mine.astype(jnp.bfloat16).astype(jnp.float32)
            + other.astype(jnp.bfloat16).astype(jnp.float32)
        ).astype(jnp.bfloat16)
        returned = lax.all_to_all(
            both.reshape((2 * expert_count,) + block_shape),
            ("req", "exp"),
            split_axis=0,
            concat_axis=0,
            tiled=True,
        )
        slot_values = returned.reshape(-1, model_width).astype(jnp.float32)
        moe_sum = moe_sum + jnp.dot(
            combine[:, chunk * chunk_total:(chunk + 1) * chunk_total],
            slot_values,
            precision=lax.Precision.HIGHEST,
            preferred_element_type=jnp.float32,
        )
    layer_out = (residual + moe_sum).astype(jnp.bfloat16)
    return (
        layer_out,
        key_rows.reshape(group_rows, local_width),
        value_rows.reshape(group_rows, local_width),
    )


def solution(mesh):
    return jax.shard_map(
        on_device,
        mesh=mesh,
        in_specs=(
            P(("req", "exp"), None),
            P(),
            P(None, None, "exp"),
            P("exp", None),
            P("req", "exp", None, None),
            P("req", None),
            P("req", None),
            P(),
            P(("req", "exp"), None),
            P(("req", "exp"), None),
            P(("req", "exp"), None, None),
            P(("req", "exp"), None, None),
            P(("req", "exp"), None, None),
        ),
        out_specs=(P(("req", "exp"), None), P("req", "exp"), P("req", "exp")),
        check_vma=False,
    )
```

```python
import jax
import jax.numpy as jnp
from jax import lax
from jax.sharding import PartitionSpec as P

HD = 128
PAGE = 16


eps_norm = 1e-06
rope_base = 10000.0


def rms_scale(inputs, gains_vec):
    return (
        inputs * lax.rsqrt(jnp.mean(inputs * inputs, axis=-1, keepdims=True) + eps_norm) * gains_vec
    )


def positions_of(group_lengths, tok_count, offset):
    end_marks = jnp.cumsum(group_lengths)
    places = jnp.arange(tok_count, dtype=jnp.int32)
    request = jnp.sum((places[:, None] >= end_marks[None, :]).astype(jnp.int32), axis=1)
    starts = end_marks - group_lengths
    onehot = (
        request[:, None] == jnp.arange(group_lengths.shape[0], dtype=jnp.int32)[None, :]
    ).astype(jnp.int32)
    first_place = jnp.sum(onehot * starts[None, :], axis=1)
    return (request, places - first_place + offset)


def rotate(inputs, places):
    half_size = inputs.shape[-1] // 2
    frequency = rope_base ** (-jnp.arange(half_size, dtype=jnp.float32) * 2.0 / inputs.shape[-1])
    angles = places.astype(jnp.float32)[:, None] * frequency[None, :]
    cosine = jnp.cos(angles)[:, None, :]
    sine_part = jnp.sin(angles)[:, None, :]
    lower = inputs[..., :half_size]
    upper = inputs[..., half_size:]
    return jnp.concatenate(
        [lower * cosine - upper * sine_part, upper * cosine + lower * sine_part], axis=-1
    )


def place_routes(block_routes, expert_count, capacity):
    flat_routes = block_routes.reshape(-1)
    entries = flat_routes.shape[0]
    onehot = (flat_routes[:, None] == jnp.arange(expert_count, dtype=jnp.int32)[None, :]).astype(
        jnp.bfloat16
    )
    rows_i = jnp.arange(entries, dtype=jnp.int32)
    earlier = (rows_i[None, :] < rows_i[:, None]).astype(jnp.bfloat16)
    before = jnp.dot(earlier, onehot, preferred_element_type=jnp.float32)
    slot_rank = jnp.sum(before * onehot.astype(jnp.float32), axis=1).astype(jnp.int32)
    return flat_routes * capacity + slot_rank


def aligned_block(size):
    for rows in (16, 8):
        if size % (rows * 128) == 0:
            return (rows, size // rows)
    return (1, size)


def half_apply(flat_rows, gate_mat, up_mat, down_mat):
    gate_proj = jnp.dot(flat_rows, gate_mat, preferred_element_type=jnp.float32)
    up_proj = jnp.dot(flat_rows, up_mat, preferred_element_type=jnp.float32)
    activated = (jax.nn.silu(gate_proj) * up_proj).astype(jnp.bfloat16)
    return jnp.dot(activated, down_mat, preferred_element_type=jnp.float32).astype(jnp.bfloat16)


def on_device(
    hidden,
    norm_attn,
    qkv_weight,
    out_weight,
    prefix_pool,
    page_table,
    suffix_lengths,
    norm_moe,
    routes,
    route_weights,
    expert_gate,
    expert_up,
    expert_down,
):
    tok_rows, model_width = hidden.shape
    holders = lax.axis_size("exp")
    head_dim = HD
    local_width = qkv_weight.shape[2]
    local_heads = local_width // head_dim
    partner = [(i, i ^ 1) for i in range(holders)]
    other_gate = lax.ppermute(expert_gate[0], "exp", partner)
    other_up = lax.ppermute(expert_up[0], "exp", partner)
    other_down = lax.ppermute(expert_down[0], "exp", partner)
    hidden_f = hidden.astype(jnp.float32)
    normed = rms_scale(hidden_f, norm_attn).astype(jnp.bfloat16)
    projected = jnp.einsum(
        "rd,cdh->rch",
        lax.all_gather(normed, "exp", axis=0, tiled=True),
        qkv_weight,
        preferred_element_type=jnp.float32,
    )
    group_rows = projected.shape[0]
    prefix_len = page_table.shape[1] * PAGE
    request, places = positions_of(suffix_lengths[0], group_rows, prefix_len)
    projected = projected.reshape(group_rows, 3, local_heads, head_dim)
    queries = rotate(projected[:, 0], places).astype(jnp.bfloat16)
    key_rows = rotate(projected[:, 1], places).astype(jnp.bfloat16)
    value_rows = projected[:, 2].astype(jnp.bfloat16)
    page_rows = page_table[0]
    own_pages = prefix_pool.shape[1]
    own_first = lax.axis_index("exp") * own_pages
    named = jnp.any(
        page_rows[None, :] == own_first + jnp.arange(own_pages, dtype=jnp.int32)[:, None],
        axis=1,
    )
    order = jnp.argsort(jnp.where(named, 0, 1).astype(jnp.int32), stable=True)
    named_pages = jnp.take(prefix_pool[0], order[: own_pages // 2], axis=0, mode="clip")
    page_data = lax.all_to_all(named_pages, "exp", split_axis=2, concat_axis=0, tiled=True)
    page_data = page_data.reshape(-1, local_heads, 2, head_dim)
    prefix_keys = page_data[:, :, 0]
    prefix_values = page_data[:, :, 1]
    score_scale = head_dim ** (-0.5)
    block_rows = min(512, group_rows)
    block_count = group_rows // block_rows

    def block_attend(operands):
        block_queries, block_requests = operands
        prefix_scores = (
            jnp.einsum(
                "qhd,khd->hqk", block_queries, prefix_keys, preferred_element_type=jnp.float32
            )
            * score_scale
        )
        suffix_scores = (
            jnp.einsum("qhd,khd->hqk", block_queries, key_rows, preferred_element_type=jnp.float32)
            * score_scale
        )
        same_request = block_requests[:, None] == request[None, :]
        suffix_scores = jnp.where(same_request[None], suffix_scores, -1e30)
        row_max = jnp.maximum(
            jnp.max(prefix_scores, axis=2, keepdims=True),
            jnp.max(suffix_scores, axis=2, keepdims=True),
        )
        prefix_weights = jnp.exp(prefix_scores - row_max)
        suffix_weights = jnp.exp(suffix_scores - row_max)
        denominator = jnp.sum(prefix_weights, axis=2) + jnp.sum(suffix_weights, axis=2)
        weighted = jnp.einsum(
            "hqk,khd->qhd",
            prefix_weights.astype(jnp.bfloat16),
            prefix_values,
            preferred_element_type=jnp.float32,
        )
        weighted = weighted + jnp.einsum(
            "hqk,khd->qhd",
            suffix_weights.astype(jnp.bfloat16),
            value_rows,
            preferred_element_type=jnp.float32,
        )
        return (weighted / jnp.transpose(denominator)[:, :, None]).astype(jnp.bfloat16)

    attended = lax.map(
        block_attend,
        (
            queries.reshape(block_count, block_rows, local_heads, head_dim),
            request.reshape(block_count, block_rows),
        ),
    )
    heads_out = attended.reshape(group_rows, local_width)
    token_heads = lax.all_to_all(
        heads_out.reshape(holders, tok_rows, local_width), "exp", split_axis=0, concat_axis=0,
        tiled=True,
    )
    half_cols = model_width // 2
    column_parts = []
    for column_start in (0, half_cols):
        weight_part = lax.all_gather(
            out_weight[:, column_start:column_start + half_cols], "exp", axis=0, tiled=True
        )
        attn_part = jnp.zeros((tok_rows, half_cols), jnp.float32)
        for part_index in range(holders):
            partial_sum = jnp.dot(
                token_heads[part_index],
                weight_part[part_index * local_width:(part_index + 1) * local_width],
                preferred_element_type=jnp.float32,
            )
            attn_part = attn_part + partial_sum.astype(jnp.bfloat16).astype(jnp.float32)
        column_parts.append(attn_part)
    residual = hidden_f + jnp.concatenate(column_parts, axis=1)
    normed_moe = rms_scale(residual, norm_moe).astype(jnp.bfloat16)
    req_count = lax.axis_size("req")
    expert_count = req_count * holders // 2
    route_count = routes.shape[1]
    capacity = max(2, tok_rows * route_count * 5 // (4 * expert_count))
    assert capacity % 2 == 0
    slot_total = expert_count * capacity
    slot_of = place_routes(routes, expert_count, capacity)
    chunks = 2 if capacity % 4 == 0 else 1
    chunk_slots = capacity // 2 // chunks
    chunk_total = 2 * expert_count * chunk_slots
    expert_of, rank_of = slot_of // capacity, slot_of % capacity
    core_of, within = rank_of // (capacity // 2), rank_of % (capacity // 2)
    slot_of = (
        within // chunk_slots * chunk_total
        + (expert_of * 2 + core_of) * chunk_slots
        + within % chunk_slots
    )
    slot_hits = (slot_of[:, None] == jnp.arange(slot_total, dtype=jnp.int32)[None, :]).reshape(
        tok_rows, route_count, slot_total
    )
    dispatch = jnp.sum(slot_hits.astype(jnp.int32), axis=1).astype(jnp.bfloat16)
    send_rows = jnp.einsum(
        "ts,td->sd", dispatch, normed_moe, preferred_element_type=jnp.float32
    ).astype(jnp.bfloat16)
    block_shape = aligned_block(chunk_slots * model_width)
    combine = jnp.sum(slot_hits.astype(jnp.float32) * route_weights[:, :, None], axis=1)
    hidden_half = expert_gate.shape[2]
    gate_up_mat = jnp.concatenate([expert_gate[0], expert_up[0], other_gate, other_up], axis=1)
    moe_sum = jnp.zeros((tok_rows, model_width), jnp.float32)
    for chunk in range(chunks):
        chunk_rows = send_rows[chunk * chunk_total:(chunk + 1) * chunk_total]
        chunk_rows = chunk_rows.reshape((2 * expert_count,) + block_shape)
        arrived = lax.all_to_all(
            chunk_rows, ("req", "exp"), split_axis=0, concat_axis=0, tiled=True
        )
        flat_rows = arrived.reshape(-1, model_width)
        gate_up = jnp.dot(flat_rows, gate_up_mat, preferred_element_type=jnp.float32)
        gate_up = gate_up.reshape(-1, 2, 2, hidden_half)
        inner = (jax.nn.silu(gate_up[:, :, 0]) * gate_up[:, :, 1]).astype(jnp.bfloat16)
        mine = jnp.dot(inner[:, 0], expert_down[0], preferred_element_type=jnp.float32)
        other = jnp.dot(inner[:, 1], other_down, preferred_element_type=jnp.float32)
        both = (
            mine.astype(jnp.bfloat16).astype(jnp.float32)
            + other.astype(jnp.bfloat16).astype(jnp.float32)
        ).astype(jnp.bfloat16)
        returned = lax.all_to_all(
            both.reshape((2 * expert_count,) + block_shape),
            ("req", "exp"),
            split_axis=0,
            concat_axis=0,
            tiled=True,
        )
        slot_values = returned.reshape(-1, model_width).astype(jnp.float32)
        moe_sum = moe_sum + jnp.dot(
            combine[:, chunk * chunk_total:(chunk + 1) * chunk_total],
            slot_values,
            precision=lax.Precision.HIGHEST,
            preferred_element_type=jnp.float32,
        )
    layer_out = (residual + moe_sum).astype(jnp.bfloat16)
    return (
        layer_out,
        key_rows.reshape(group_rows, local_width),
        value_rows.reshape(group_rows, local_width),
    )


def solution(mesh):
    return jax.shard_map(
        on_device,
        mesh=mesh,
        in_specs=(
            P(("req", "exp"), None),
            P(),
            P(None, None, "exp"),
            P("exp", None),
            P("req", "exp", None, None),
            P("req", None),
            P("req", None),
            P(),
            P(("req", "exp"), None),
            P(("req", "exp"), None),
            P(("req", "exp"), None, None),
            P(("req", "exp"), None, None),
            P(("req", "exp"), None, None),
        ),
        out_specs=(P(("req", "exp"), None), P("req", "exp"), P("req", "exp")),
        check_vma=False,
    )
```
